256 devices in a mesh: stn: 64 (over y, z, core), sec: 4 (over x).
Axes of the slice: x: 4, y: 4, z: 8, core: 2. Of those that a mesh axis runs over, the one named last changes fastest.
Arguments:
- voltages: bfloat16 [2, 1024, 569344], P(None, ('stn', 'sec')), may hold values from -6 to 6
- fir_taps: float32 [12, 4096], replicated, may hold values from -1.75 to 1.75
- cor_channels: int32 [256], replicated, may hold values from 0 to 4095, as said below
- beam_channels: int32 [256], replicated, may hold values from 1 to 4094, as said below
- cor_gain: float32 [256], replicated, as said below
- beam_gain: float32 [256], replicated, as said below
- beam_stations: int32 [16, 512], replicated, may hold values from 0 to 511
- beam_codes: int32 [16, 512], replicated, may hold values from 0 to 255
Outputs:
- visibilities: bfloat16 [256, 2, 1024, 1024], P(('stn', 'sec'))
- beams: bfloat16 [256, 16, 2, 256], P(('stn', 'sec'))
The draws below stay inside these ranges and needn't reach their ends.
Inputs may be any that keep to these rules, and one draw needn't show every extreme that they name: cor_channels and beam_channels together are 512 distinct transform channels. None of beam_channels appears in cor_channels. `cor_gain`: positive. `beam_gain`: positive.
All inputs are finite; a program needn't handle non-finite values.
Results may differ from the reference program's by a relative error of at most 0.0085.
Values may be sent and summed in bfloat16 or wider, within the bound.
No kernel may reach another device: no remote copies, remote signals or barrier semaphores. Data moves between devices by JAX's collectives and lax.ppermute only.
A program may use at most 128 MiB of HBM per device.

```python
import math
import jax
import jax.numpy as jnp
from jax import lax

STATIONS = 512
NFFT = 4096
TAPS = 12
NBEAM = 16
BEAM_STN = 512
SPECTRA = 128
INPUTS = 1024
FRAMES = 139
NCOR = 256
NBC = 256


def channel_lists(key):
    middle = (jax.random.permutation(jax.random.fold_in(key, 7), NFFT - 4) + 2).astype(jnp.int32)
    cor_ends = jnp.array([0, NFFT - 1], dtype=jnp.int32)
    beam_ends = jnp.array([1, NFFT - 2], dtype=jnp.int32)
    cor_list = jnp.concatenate([cor_ends, middle[:NCOR - 2]])
    beam_list = jnp.concatenate([beam_ends, middle[NCOR - 2:NCOR - 2 + NBC - 2]])
    cor_order = jax.random.permutation(jax.random.fold_in(key, 17), NCOR)
    beam_order = jax.random.permutation(jax.random.fold_in(key, 19), NBC)
    return (cor_list[cor_order].astype(jnp.int32), beam_list[beam_order].astype(jnp.int32))


def draw_cor_channels(key, part):
    return channel_lists(key)[0]


def draw_beam_channels(key, part):
    return channel_lists(key)[1]


def rising_gain(key, salt, length):
    position = jnp.arange(length, dtype=jnp.float32) / max(length - 1, 1)
    baseline = jnp.exp(position * math.log(3.0))
    subkey = jax.random.fold_in(key, salt)
    factor = jnp.exp(jax.random.uniform(subkey, (length,), jnp.float32, 0.0, math.log(3.3)))
    return baseline * factor


def draw_cor_gain(key, part):
    return rising_gain(key, 11, NCOR)


def draw_beam_gain(key, part):
    return rising_gain(key, 13, NBC)


def with_ends(result, stream_key, low, largest):
    place = [jax.random.randint(jax.random.fold_in(stream_key, axis), (), 0, length) for axis, length in enumerate(result.shape)]
    widest = result.shape.index(max(result.shape))
    neighbour = place[:widest] + [(place[widest] + 1) % result.shape[widest]] + place[widest + 1:]
    return result.at[tuple(place)].set(low).at[tuple(neighbour)].set(largest)


def steps_of(rng, dims, cuts, smallest, largest):
    def one(dim, shards_of):
        steps = jax.random.uniform(jax.random.fold_in(jax.random.fold_in(rng, 6), dim), (shards_of,), jnp.float32, smallest / len(cuts), largest / len(cuts))
        return jnp.repeat(jnp.exp(steps), dims[dim] // shards_of).reshape((-1,) + (1,) * (len(dims) - dim - 1))

    loudness = one(*cuts[0])
    for cut in cuts[1:]:
        loudness = loudness * one(*cut)
    return loudness


def normal_values(stream_key, dims, spread, reach, shards=(), kind=jnp.bfloat16):
    values = spread * jax.random.normal(stream_key, dims, jnp.float32)
    if shards:
        values = values * steps_of(stream_key, dims, shards, -0.22, 0.18)
    return jnp.clip(values, -reach, reach).astype(kind)


def setup_inputs(seed: int = 0) -> dict:
    arg_keys = jax.random.split(jax.random.key(seed), 9)
    return {
        "voltages": normal_values(arg_keys[0], (2, INPUTS, FRAMES * NFFT), 1.0, 6.0, ((1, 256),)),
        "fir_taps": normal_values(arg_keys[1], (TAPS, NFFT), TAPS ** -0.5, 1.75, (), jnp.float32),
        "cor_channels": draw_cor_channels(jax.random.fold_in(arg_keys[8], 71), 0),
        "beam_channels": draw_beam_channels(jax.random.fold_in(arg_keys[8], 71), 0),
        "cor_gain": draw_cor_gain(jax.random.fold_in(arg_keys[8], 71), 0),
        "beam_gain": draw_beam_gain(jax.random.fold_in(arg_keys[8], 71), 0),
        "beam_stations": with_ends(jax.random.randint(arg_keys[6], (NBEAM, BEAM_STN), 0, STATIONS), jax.random.fold_in(arg_keys[6], 1), 0, STATIONS - 1).astype(jnp.int32),
        "beam_codes": with_ends(jax.random.randint(arg_keys[7], (NBEAM, BEAM_STN), 0, 256), jax.random.fold_in(arg_keys[7], 1), 0, 255).astype(jnp.int32),
    }


epsilon = 1e-05

def make_tables(channel_of, points):
    sample_index = jnp.arange(points, dtype=jnp.int32)
    phase_turns = channel_of[:, None] * sample_index[None, :] % points
    phase_angle = phase_turns.astype(jnp.float32) * (2.0 * math.pi / points)
    table_scale = 1.0 / math.sqrt(points)
    cos_table = (jnp.cos(phase_angle) * table_scale).astype(jnp.bfloat16)
    sin_table = (jnp.sin(phase_angle) * table_scale).astype(jnp.bfloat16)
    return (cos_table, sin_table)

def make_weights(beam_stations, beam_codes, stations):
    station_ids = jnp.arange(stations, dtype=jnp.int32)
    onehot = (beam_stations[:, :, None] == station_ids[None, None, :]).astype(jnp.float32)
    amplitude = (1 + beam_codes // 64).astype(jnp.float32)
    phase_angle = (beam_codes % 64).astype(jnp.float32) * (2.0 * math.pi / 64.0)
    weight_re = jnp.einsum('bk,bks->bs', amplitude * jnp.cos(phase_angle), onehot)
    weight_im = jnp.einsum('bk,bks->bs', amplitude * jnp.sin(phase_angle), onehot)
    return (weight_re.astype(jnp.bfloat16), weight_im.astype(jnp.bfloat16))

def polyphase(in_block, fir_taps, spectra):
    tap_count, points = fir_taps.shape
    framed = in_block.reshape(in_block.shape[0], in_block.shape[1], -1, points)
    summed = jnp.zeros((framed.shape[0], framed.shape[1], spectra, points), jnp.float32)
    for tap_index in range(tap_count):
        summed = summed + fir_taps[tap_index] * framed[:, :, tap_index:tap_index + spectra, :].astype(jnp.float32)
    return summed.astype(jnp.bfloat16)

def spectrum(filtered, cos_table, sin_table, slot_gain):
    inputs_here, spectra, points = (filtered.shape[1], filtered.shape[2], filtered.shape[3])
    real_rows = filtered[0].reshape(inputs_here * spectra, points)
    imag_rows = filtered[1].reshape(inputs_here * spectra, points)
    spec_re = jnp.dot(cos_table, real_rows.T, preferred_element_type=jnp.float32) + jnp.dot(sin_table, imag_rows.T, preferred_element_type=jnp.float32)
    spec_im = jnp.dot(cos_table, imag_rows.T, preferred_element_type=jnp.float32) - jnp.dot(sin_table, real_rows.T, preferred_element_type=jnp.float32)
    combined = jnp.concatenate([spec_re.reshape(-1, inputs_here, spectra), spec_im.reshape(-1, inputs_here, spectra)], axis=2)
    return (combined * slot_gain[:, None, None]).astype(jnp.bfloat16)

def form_beams(beam_data, weight_re, weight_im):
    spectra = beam_data.shape[2] // 2
    samples = beam_data.astype(jnp.float32).reshape(beam_data.shape[0], -1, 2, beam_data.shape[2])
    with_re = jnp.einsum('bs,jspt->jbpt', weight_re.astype(jnp.float32), samples)
    with_im = jnp.einsum('bs,jspt->jbpt', weight_im.astype(jnp.float32), samples)
    out_re = with_re[..., :spectra] - with_im[..., spectra:]
    out_im = with_re[..., spectra:] + with_im[..., :spectra]
    return jnp.concatenate([out_re, out_im], axis=3)

def reference(voltages, fir_taps, cor_channels, beam_channels, cor_gain, beam_gain, beam_stations, beam_codes):
    channel_of = jnp.concatenate([cor_channels, beam_channels])
    slot_gain = jnp.concatenate([cor_gain, beam_gain])
    cos_table, sin_table = make_tables(channel_of, NFFT)
    block_inputs = 32
    block_count = INPUTS // block_inputs

    def one_block(block_index):
        first_input = (block_index * block_inputs).astype(jnp.int32)
        portion = lax.dynamic_slice_in_dim(voltages, first_input, block_inputs, 1)
        return spectrum(polyphase(portion, fir_taps, SPECTRA), cos_table, sin_table, slot_gain)
    blocked = lax.map(one_block, jnp.arange(block_count, dtype=jnp.int32))
    spectra = jnp.transpose(blocked, (1, 0, 2, 3)).reshape(NCOR + NBC, INPUTS, 2 * SPECTRA)

    def correlate(matrix):
        swapped = jnp.concatenate([matrix[:, SPECTRA:], -matrix[:, :SPECTRA]], axis=1)
        vis_re = jnp.dot(matrix, matrix.T, preferred_element_type=jnp.float32) / SPECTRA
        vis_im = jnp.dot(swapped, matrix.T, preferred_element_type=jnp.float32) / SPECTRA
        return jnp.stack([vis_re, vis_im]).astype(jnp.bfloat16)
    visibilities = lax.map(correlate, spectra[:NCOR])
    weight_re, weight_im = make_weights(beam_stations, beam_codes, STATIONS)
    raw_beams = form_beams(spectra[NCOR:], weight_re, weight_im)
    entry_count = raw_beams.shape[0] * raw_beams.shape[2] * raw_beams.shape[3]
    beam_power = lax.optimization_barrier(jnp.sum(raw_beams * raw_beams, axis=(0, 2, 3))) / entry_count
    beams = (raw_beams * lax.rsqrt(beam_power + epsilon)[None, :, None, None]).astype(jnp.bfloat16)
    return (visibilities, beams)
```

```python
import math

import jax
import jax.numpy as jnp
from jax import lax
from jax.sharding import PartitionSpec as P

STATIONS = 512


epsilon = 1e-05

STN_AXES = ("y", "z", "core")
PHYSICAL_AXES = ("core", "x", "y", "z")


def make_tables(channel_of, points):
    outer = 64
    inner = points // outer
    step = 2.0 * math.pi / points
    a_index = jnp.arange(inner, dtype=jnp.int32)
    b_index = jnp.arange(outer, dtype=jnp.int32)
    a_turns = (channel_of[:, None] * a_index[None, :] % inner) * outer
    b_turns = channel_of[:, None] * b_index[None, :] % points
    a_angle = a_turns.astype(jnp.float32) * step
    b_angle = b_turns.astype(jnp.float32) * step
    ca, sa = jnp.cos(a_angle)[:, :, None], jnp.sin(a_angle)[:, :, None]
    cb, sb = jnp.cos(b_angle)[:, None, :], jnp.sin(b_angle)[:, None, :]
    table_scale = 1.0 / math.sqrt(points)
    cos_table = ((ca * cb - sa * sb) * table_scale).astype(jnp.bfloat16)
    sin_table = ((sa * cb + ca * sb) * table_scale).astype(jnp.bfloat16)
    slots = channel_of.shape[0]
    return (cos_table.reshape(slots, points), sin_table.reshape(slots, points))


def make_weights(beam_stations, beam_codes, stations):
    station_ids = jnp.arange(stations, dtype=jnp.int32)
    onehot = (beam_stations[:, :, None] == station_ids[None, None, :]).astype(jnp.float32)
    amplitude = (1 + beam_codes // 64).astype(jnp.float32)
    phase_angle = (beam_codes % 64).astype(jnp.float32) * (2.0 * math.pi / 64.0)
    weight_re = jnp.einsum("bk,bks->bs", amplitude * jnp.cos(phase_angle), onehot)
    weight_im = jnp.einsum("bk,bks->bs", amplitude * jnp.sin(phase_angle), onehot)
    return (weight_re.astype(jnp.bfloat16), weight_im.astype(jnp.bfloat16))


def polyphase(in_block, fir_taps, spectra):
    tap_count, points = fir_taps.shape
    framed = in_block.reshape(in_block.shape[0], in_block.shape[1], -1, points)
    summed = jnp.zeros((framed.shape[0], framed.shape[1], spectra, points), jnp.float32)
    for tap_index in range(tap_count):
        summed = summed + fir_taps[tap_index] * framed[
            :, :, tap_index : tap_index + spectra, :
        ].astype(jnp.float32)
    return summed.astype(jnp.bfloat16)


def contract(left_rows, right_rows):
    contract_dims = (((1,), (1,)), ((), ()))
    return lax.dot_general(left_rows, right_rows, contract_dims, preferred_element_type=jnp.float32)


def spectrum(filtered, cos_table, sin_table, slot_gain):
    inputs_here, spectra, points = (filtered.shape[1], filtered.shape[2], filtered.shape[3])
    rows = inputs_here * spectra
    slots = cos_table.shape[0]
    tables = jnp.concatenate([cos_table, sin_table], axis=0)
    products = contract(tables, filtered.reshape(2 * rows, points))
    cos_re, cos_im = products[:slots, :rows], products[:slots, rows:]
    sin_re, sin_im = products[slots:, :rows], products[slots:, rows:]
    spec_re = cos_re + sin_im
    spec_im = cos_im - sin_re
    combined = jnp.concatenate(
        [spec_re.reshape(-1, inputs_here, spectra), spec_im.reshape(-1, inputs_here, spectra)],
        axis=2,
    )
    return (combined * slot_gain[:, None, None]).astype(jnp.bfloat16)


def form_beams(beam_data, weight_re, weight_im):
    spectra = beam_data.shape[2] // 2
    samples = beam_data.reshape(beam_data.shape[0], -1, 2, beam_data.shape[2])
    with_re = jnp.einsum("bs,jspt->jbpt", weight_re, samples, preferred_element_type=jnp.float32)
    with_im = jnp.einsum("bs,jspt->jbpt", weight_im, samples, preferred_element_type=jnp.float32)
    out_re = with_re[..., :spectra] - with_im[..., spectra:]
    out_im = with_re[..., spectra:] + with_im[..., :spectra]
    return jnp.concatenate([out_re, out_im], axis=3)


def per_device(
    voltages, fir_taps, cor_channels, beam_channels, cor_gain, beam_gain, beam_stations, beam_codes
):
    tap_count, points = fir_taps.shape
    stn_count = lax.axis_size(STN_AXES)
    sec_count = lax.axis_size("x")
    device_count = stn_count * sec_count
    inputs_here = voltages.shape[1]
    spectra = voltages.shape[2] // points - tap_count + 1
    filtered = polyphase(voltages, fir_taps, spectra)
    channel_of = jnp.concatenate([cor_channels, beam_channels])
    slot_gain = jnp.concatenate([cor_gain, beam_gain])
    cos_table, sin_table = lax.optimization_barrier(make_tables(channel_of, points))
    weight_re, weight_im = make_weights(beam_stations, beam_codes, STATIONS)
    spectra_all = spectrum(filtered, cos_table, sin_table, slot_gain)
    outgoing = spectra_all.reshape(2, stn_count, sec_count, 1, 1, inputs_here, 2 * spectra)
    turned = lax.all_to_all(
        lax.all_to_all(outgoing, STN_AXES, split_axis=1, concat_axis=3, tiled=True),
        "x",
        split_axis=2,
        concat_axis=4,
        tiled=True,
    )
    received = turned.reshape(2, device_count * inputs_here, 2 * spectra)
    cor_data = received[0]
    beam_data = received[1:2]
    swapped = jnp.concatenate([cor_data[:, spectra:], -cor_data[:, :spectra]], axis=1)
    vis_re = contract(cor_data, cor_data) / spectra
    vis_im = contract(swapped, cor_data) / spectra
    visibilities = jnp.stack([vis_re, vis_im])[None].astype(jnp.bfloat16)
    raw_beams = form_beams(beam_data, weight_re, weight_im)
    local_power = jnp.sum(raw_beams * raw_beams, axis=(0, 2, 3))
    summed_power = local_power
    for axis in PHYSICAL_AXES:
        summed_power = lax.psum(summed_power, axis)
    beam_power = summed_power / (device_count * raw_beams.shape[2] * raw_beams.shape[3])
    beams = (raw_beams * lax.rsqrt(beam_power + epsilon)[None, :, None, None]).astype(jnp.bfloat16)
    return (visibilities, beams)


def solution(mesh):
    stn_count, sec_count = mesh.devices.shape
    cores = 2
    y_count = 4
    z_count = stn_count // (y_count * cores)
    devices = mesh.devices.reshape(y_count, z_count, cores, sec_count)
    fine = jax.sharding.Mesh(devices, ("y", "z", "core", "x"))
    spread = ("y", "z", "core", "x")
    in_specs = (P(None, spread, None), P(), P(), P(), P(), P(), P(), P())
    out_specs = (P(spread, None, None, None), P(spread, None, None, None))
    return jax.shard_map(
        per_device, mesh=fine, in_specs=in_specs, out_specs=out_specs, check_vma=False
    )
```

```python
import math

import jax
import jax.numpy as jnp
from jax import lax
from jax.experimental import pallas as pl
from jax.sharding import PartitionSpec as P

STATIONS = 512


epsilon = 1e-05

STN_AXES = ("y", "z", "core")
PHYSICAL_AXES = ("core", "x", "y", "z")


def make_tables(channel_of, points):
    outer = 64
    inner = points // outer
    step = 2.0 * math.pi / points
    a_index = jnp.arange(inner, dtype=jnp.int32)
    b_index = jnp.arange(outer, dtype=jnp.int32)
    a_turns = (channel_of[:, None] * a_index[None, :] % inner) * outer
    b_turns = channel_of[:, None] * b_index[None, :] % points
    a_angle = a_turns.astype(jnp.float32) * step
    b_angle = b_turns.astype(jnp.float32) * step
    ca, sa = jnp.cos(a_angle)[:, :, None], jnp.sin(a_angle)[:, :, None]
    cb, sb = jnp.cos(b_angle)[:, None, :], jnp.sin(b_angle)[:, None, :]
    table_scale = 1.0 / math.sqrt(points)
    cos_table = ((ca * cb - sa * sb) * table_scale).astype(jnp.bfloat16)
    sin_table = ((sa * cb + ca * sb) * table_scale).astype(jnp.bfloat16)
    slots = channel_of.shape[0]
    return (cos_table.reshape(slots, points), sin_table.reshape(slots, points))


def make_weights(beam_stations, beam_codes, stations):
    station_ids = jnp.arange(stations, dtype=jnp.int32)
    onehot = (beam_stations[:, :, None] == station_ids[None, None, :]).astype(jnp.float32)
    amplitude = (1 + beam_codes // 64).astype(jnp.float32)
    phase_angle = (beam_codes % 64).astype(jnp.float32) * (2.0 * math.pi / 64.0)
    weight_re = jnp.einsum("bk,bks->bs", amplitude * jnp.cos(phase_angle), onehot)
    weight_im = jnp.einsum("bk,bks->bs", amplitude * jnp.sin(phase_angle), onehot)
    return (weight_re.astype(jnp.bfloat16), weight_im.astype(jnp.bfloat16))


def fir_kernel(x_ref, h_ref, o_ref):
    tap_count = h_ref.shape[0]
    rows = x_ref.shape[1]
    width = h_ref.shape[1]
    taps = [jnp.broadcast_to(h_ref[pl.ds(t, 1), :], (rows, width)) for t in range(tap_count)]

    def body(j, carry):
        first = 2 * j
        frames = [x_ref[first + f] for f in range(tap_count + 1)]
        pair = []
        for k in range(2):
            acc = taps[0] * frames[k]
            for t in range(1, tap_count):
                acc = acc + taps[t] * frames[k + t]
            pair.append(acc)
        o_ref[j] = jnp.concatenate(pair, axis=0).astype(o_ref.dtype)
        return carry

    lax.fori_loop(0, o_ref.shape[0], body, 0)


def polyphase(in_block, fir_taps, spectra):
    tap_count, points = fir_taps.shape
    components, inputs_here = in_block.shape[0], in_block.shape[1]
    rows = components * inputs_here
    frames = in_block.shape[2] // points
    framed = in_block.reshape(components, inputs_here, frames, points)
    framed = jnp.transpose(framed, (2, 0, 1, 3)).reshape(frames, rows, points)
    framed = framed.astype(jnp.float32)
    width = 256
    return pl.pallas_call(
        fir_kernel,
        grid=(points // width,),
        in_specs=[
            pl.BlockSpec((frames, rows, width), lambda n: (0, 0, n)),
            pl.BlockSpec((tap_count, width), lambda n: (0, n)),
        ],
        out_specs=pl.BlockSpec((spectra // 2, 2 * rows, width), lambda n: (0, 0, n)),
        out_shape=jax.ShapeDtypeStruct((spectra // 2, 2 * rows, points), jnp.bfloat16),
    )(framed, fir_taps)


def contract(left_rows, right_rows):
    contract_dims = (((1,), (1,)), ((), ()))
    return lax.dot_general(left_rows, right_rows, contract_dims, preferred_element_type=jnp.float32)


def spectrum(filtered, cos_table, sin_table, slot_gain, inputs_here):
    points = filtered.shape[2]
    spectra = 2 * filtered.shape[0]
    slots = cos_table.shape[0]
    tables = jnp.concatenate([cos_table, sin_table], axis=0)
    products = contract(tables, filtered.reshape(-1, points))
    products = products.reshape(2, slots, spectra, 2, inputs_here)
    cos_re, cos_im = products[0, :, :, 0], products[0, :, :, 1]
    sin_re, sin_im = products[1, :, :, 0], products[1, :, :, 1]
    spec_re = jnp.transpose(cos_re + sin_im, (0, 2, 1))
    spec_im = jnp.transpose(cos_im - sin_re, (0, 2, 1))
    combined = jnp.concatenate([spec_re, spec_im], axis=2)
    return (combined * slot_gain[:, None, None]).astype(jnp.bfloat16)


def form_beams(beam_data, weight_re, weight_im):
    spectra = beam_data.shape[2] // 2
    samples = beam_data.reshape(beam_data.shape[0], -1, 2, beam_data.shape[2])
    with_re = jnp.einsum("bs,jspt->jbpt", weight_re, samples, preferred_element_type=jnp.float32)
    with_im = jnp.einsum("bs,jspt->jbpt", weight_im, samples, preferred_element_type=jnp.float32)
    out_re = with_re[..., :spectra] - with_im[..., spectra:]
    out_im = with_re[..., spectra:] + with_im[..., :spectra]
    return jnp.concatenate([out_re, out_im], axis=3)


def per_device(
    voltages, fir_taps, cor_channels, beam_channels, cor_gain, beam_gain, beam_stations, beam_codes
):
    tap_count, points = fir_taps.shape
    stn_count = lax.axis_size(STN_AXES)
    sec_count = lax.axis_size("x")
    device_count = stn_count * sec_count
    inputs_here = voltages.shape[1]
    spectra = voltages.shape[2] // points - tap_count + 1
    filtered = polyphase(voltages, fir_taps, spectra)
    channel_of = jnp.concatenate([cor_channels, beam_channels])
    slot_gain = jnp.concatenate([cor_gain, beam_gain])
    cos_table, sin_table = lax.optimization_barrier(make_tables(channel_of, points))
    weight_re, weight_im = make_weights(beam_stations, beam_codes, STATIONS)
    spectra_all = spectrum(filtered, cos_table, sin_table, slot_gain, inputs_here)
    outgoing = spectra_all.reshape(2, stn_count, sec_count, 1, 1, inputs_here, 2 * spectra)
    turned = lax.all_to_all(
        lax.all_to_all(outgoing, STN_AXES, split_axis=1, concat_axis=3, tiled=True),
        "x",
        split_axis=2,
        concat_axis=4,
        tiled=True,
    )
    received = turned.reshape(2, device_count * inputs_here, 2 * spectra)
    cor_data = received[0]
    beam_data = received[1:2]
    swapped = jnp.concatenate([cor_data[:, spectra:], -cor_data[:, :spectra]], axis=1)
    vis_re = contract(cor_data, cor_data) / spectra
    vis_im = contract(swapped, cor_data) / spectra
    visibilities = jnp.stack([vis_re, vis_im])[None].astype(jnp.bfloat16)
    raw_beams = form_beams(beam_data, weight_re, weight_im)
    local_power = jnp.sum(raw_beams * raw_beams, axis=(0, 2, 3))
    summed_power = local_power
    for axis in PHYSICAL_AXES:
        summed_power = lax.psum(summed_power, axis)
    beam_power = summed_power / (device_count * raw_beams.shape[2] * raw_beams.shape[3])
    beams = (raw_beams * lax.rsqrt(beam_power + epsilon)[None, :, None, None]).astype(jnp.bfloat16)
    return (visibilities, beams)


def solution(mesh):
    stn_count, sec_count = mesh.devices.shape
    cores = 2
    y_count = 4
    z_count = stn_count // (y_count * cores)
    devices = mesh.devices.reshape(y_count, z_count, cores, sec_count)
    fine = jax.sharding.Mesh(devices, ("y", "z", "core", "x"))
    spread = ("y", "z", "core", "x")
    in_specs = (P(None, spread, None), P(), P(), P(), P(), P(), P(), P())
    out_specs = (P(spread, None, None, None), P(spread, None, None, None))
    return jax.shard_map(
        per_device, mesh=fine, in_specs=in_specs, out_specs=out_specs, check_vma=False
    )
```

```python
import math

import jax
import jax.numpy as jnp
from jax import lax
from jax.sharding import PartitionSpec as P

STATIONS = 512


epsilon = 1e-05

STN_AXES = ("y", "z", "core")
PHYSICAL_AXES = ("core", "x", "y", "z")
POWER_PAD = 65536


def make_tables(channel_of, points):
    outer = 64
    inner = points // outer
    step = 2.0 * math.pi / points
    a_index = jnp.arange(inner, dtype=jnp.int32)
    b_index = jnp.arange(outer, dtype=jnp.int32)
    a_turns = (channel_of[:, None] * a_index[None, :] % inner) * outer
    b_turns = channel_of[:, None] * b_index[None, :] % points
    a_angle = a_turns.astype(jnp.float32) * step
    b_angle = b_turns.astype(jnp.float32) * step
    ca, sa = jnp.cos(a_angle)[:, :, None], jnp.sin(a_angle)[:, :, None]
    cb, sb = jnp.cos(b_angle)[:, None, :], jnp.sin(b_angle)[:, None, :]
    table_scale = 1.0 / math.sqrt(points)
    cos_table = ((ca * cb - sa * sb) * table_scale).astype(jnp.bfloat16)
    sin_table = ((sa * cb + ca * sb) * table_scale).astype(jnp.bfloat16)
    slots = channel_of.shape[0]
    return (cos_table.reshape(slots, points), sin_table.reshape(slots, points))


def make_weights(beam_stations, beam_codes, stations):
    station_ids = jnp.arange(stations, dtype=jnp.int32)
    onehot = (beam_stations[:, :, None] == station_ids[None, None, :]).astype(jnp.float32)
    amplitude = (1 + beam_codes // 64).astype(jnp.float32)
    phase_angle = (beam_codes % 64).astype(jnp.float32) * (2.0 * math.pi / 64.0)
    weight_re = jnp.einsum("bk,bks->bs", amplitude * jnp.cos(phase_angle), onehot)
    weight_im = jnp.einsum("bk,bks->bs", amplitude * jnp.sin(phase_angle), onehot)
    return (weight_re.astype(jnp.bfloat16), weight_im.astype(jnp.bfloat16))


def polyphase(in_block, fir_taps, spectra):
    tap_count, points = fir_taps.shape
    framed = in_block.reshape(in_block.shape[0], in_block.shape[1], -1, points)
    summed = jnp.zeros((framed.shape[0], framed.shape[1], spectra, points), jnp.float32)
    for tap_index in range(tap_count):
        summed = summed + fir_taps[tap_index] * framed[
            :, :, tap_index : tap_index + spectra, :
        ].astype(jnp.float32)
    return summed.astype(jnp.bfloat16)


def contract(left_rows, right_rows):
    contract_dims = (((1,), (1,)), ((), ()))
    return lax.dot_general(left_rows, right_rows, contract_dims, preferred_element_type=jnp.float32)


def spectrum(filtered, cos_table, sin_table, slot_gain):
    inputs_here, spectra, points = (filtered.shape[1], filtered.shape[2], filtered.shape[3])
    rows = inputs_here * spectra
    slots = cos_table.shape[0]
    tables = jnp.concatenate([cos_table, sin_table], axis=0)
    products = contract(tables, filtered.reshape(2 * rows, points))
    cos_re, cos_im = products[:slots, :rows], products[:slots, rows:]
    sin_re, sin_im = products[slots:, :rows], products[slots:, rows:]
    spec_re = cos_re + sin_im
    spec_im = cos_im - sin_re
    combined = jnp.concatenate(
        [spec_re.reshape(-1, inputs_here, spectra), spec_im.reshape(-1, inputs_here, spectra)],
        axis=2,
    )
    return (combined * slot_gain[:, None, None]).astype(jnp.bfloat16)


def form_beams(beam_data, weight_re, weight_im):
    spectra = beam_data.shape[2] // 2
    samples = beam_data.reshape(beam_data.shape[0], -1, 2, beam_data.shape[2])
    with_re = jnp.einsum("bs,jspt->jbpt", weight_re, samples, preferred_element_type=jnp.float32)
    with_im = jnp.einsum("bs,jspt->jbpt", weight_im, samples, preferred_element_type=jnp.float32)
    out_re = with_re[..., :spectra] - with_im[..., spectra:]
    out_im = with_re[..., spectra:] + with_im[..., :spectra]
    return jnp.concatenate([out_re, out_im], axis=3)


def per_device(
    voltages, fir_taps, cor_channels, beam_channels, cor_gain, beam_gain, beam_stations, beam_codes
):
    tap_count, points = fir_taps.shape
    stn_count = lax.axis_size(STN_AXES)
    sec_count = lax.axis_size("x")
    device_count = stn_count * sec_count
    inputs_here = voltages.shape[1]
    spectra = voltages.shape[2] // points - tap_count + 1
    filtered = polyphase(voltages, fir_taps, spectra)
    channel_of = jnp.concatenate([cor_channels, beam_channels])
    slot_gain = jnp.concatenate([cor_gain, beam_gain])
    cos_table, sin_table = lax.optimization_barrier(make_tables(channel_of, points))
    weight_re, weight_im = make_weights(beam_stations, beam_codes, STATIONS)
    spectra_all = spectrum(filtered, cos_table, sin_table, slot_gain)
    slots = spectra_all.shape[0] // 2

    def exchange(part):
        outgoing = part.reshape(stn_count, sec_count, 1, 1, inputs_here, 2 * spectra)
        turned = lax.all_to_all(
            lax.all_to_all(outgoing, STN_AXES, split_axis=0, concat_axis=2, tiled=True),
            "x",
            split_axis=1,
            concat_axis=3,
            tiled=True,
        )
        return turned.reshape(device_count * inputs_here, 2 * spectra)

    beam_data = exchange(spectra_all[slots:])[None]
    raw_beams = form_beams(beam_data, weight_re, weight_im)
    local_power = jnp.sum(raw_beams * raw_beams, axis=(0, 2, 3))
    padded = jnp.zeros((POWER_PAD,), jnp.float32).at[: local_power.shape[0]].set(local_power)
    padded, cor_part = lax.optimization_barrier((padded, spectra_all[:slots]))
    summed_power = lax.psum(padded, PHYSICAL_AXES)[: local_power.shape[0]]
    cor_data = exchange(cor_part)
    swapped = jnp.concatenate([cor_data[:, spectra:], -cor_data[:, :spectra]], axis=1)
    vis_re = contract(cor_data, cor_data) / spectra
    vis_im = contract(swapped, cor_data) / spectra
    visibilities = jnp.stack([vis_re, vis_im])[None].astype(jnp.bfloat16)
    beam_power = summed_power / (device_count * raw_beams.shape[2] * raw_beams.shape[3])
    beams = (raw_beams * lax.rsqrt(beam_power + epsilon)[None, :, None, None]).astype(jnp.bfloat16)
    return (visibilities, beams)


def solution(mesh):
    stn_count, sec_count = mesh.devices.shape
    cores = 2
    y_count = 4
    z_count = stn_count // (y_count * cores)
    devices = mesh.devices.reshape(y_count, z_count, cores, sec_count)
    fine = jax.sharding.Mesh(devices, ("y", "z", "core", "x"))
    spread = ("y", "z", "core", "x")
    in_specs = (P(None, spread, None), P(), P(), P(), P(), P(), P(), P())
    out_specs = (P(spread, None, None, None), P(spread, None, None, None))
    return jax.shard_map(
        per_device, mesh=fine, in_specs=in_specs, out_specs=out_specs, check_vma=False
    )
```

```python
import math

import jax
import jax.numpy as jnp
from jax import lax
from jax.experimental import pallas as pl
from jax.experimental.pallas import tpu as pltpu
from jax.sharding import PartitionSpec as P

STATIONS = 512


epsilon = 1e-05

STN_AXES = ("y", "z", "core")
PHYSICAL_AXES = ("core", "x", "y", "z")


def make_tables(channel_of, points):
    outer = 64
    inner = points // outer
    step = 2.0 * math.pi / points
    a_index = jnp.arange(inner, dtype=jnp.int32)
    b_index = jnp.arange(outer, dtype=jnp.int32)
    a_turns = (channel_of[:, None] * a_index[None, :] % inner) * outer
    b_turns = channel_of[:, None] * b_index[None, :] % points
    a_angle = a_turns.astype(jnp.float32) * step
    b_angle = b_turns.astype(jnp.float32) * step
    ca, sa = jnp.cos(a_angle)[:, :, None], jnp.sin(a_angle)[:, :, None]
    cb, sb = jnp.cos(b_angle)[:, None, :], jnp.sin(b_angle)[:, None, :]
    table_scale = 1.0 / math.sqrt(points)
    cos_table = ((ca * cb - sa * sb) * table_scale).astype(jnp.bfloat16)
    sin_table = ((sa * cb + ca * sb) * table_scale).astype(jnp.bfloat16)
    slots = channel_of.shape[0]
    return (cos_table.reshape(slots, points), sin_table.reshape(slots, points))


def make_weights(beam_stations, beam_codes, stations):
    station_ids = jnp.arange(stations, dtype=jnp.int32)
    onehot = (beam_stations[:, :, None] == station_ids[None, None, :]).astype(jnp.float32)
    amplitude = (1 + beam_codes // 64).astype(jnp.float32)
    phase_angle = (beam_codes % 64).astype(jnp.float32) * (2.0 * math.pi / 64.0)
    weight_re = jnp.einsum("bk,bks->bs", amplitude * jnp.cos(phase_angle), onehot)
    weight_im = jnp.einsum("bk,bks->bs", amplitude * jnp.sin(phase_angle), onehot)
    return (weight_re.astype(jnp.bfloat16), weight_im.astype(jnp.bfloat16))


def fir_kernel(x_ref, h_ref, o_ref, xs_ref):
    tap_count = h_ref.shape[0]
    frames = x_ref.shape[2]
    spectra = o_ref.shape[2]
    lanes = 256
    xs_ref[pl.ds(0, frames), :] = x_ref[0, 0].astype(jnp.float32)

    def lane_body(lane_block, carry):
        n0 = pl.multiple_of(lane_block * lanes, lanes)
        taps = [
            jnp.broadcast_to(h_ref[pl.ds(t, 1), pl.ds(n0, lanes)], (8, lanes))
            for t in range(tap_count)
        ]
        for pair in range(spectra // 16):
            halves = []
            for half in range(2):
                s0 = 16 * pair + 8 * half
                acc = taps[0] * xs_ref[pl.ds(s0, 8), pl.ds(n0, lanes)]
                for t in range(1, tap_count):
                    acc = acc + taps[t] * xs_ref[pl.ds(s0 + t, 8), pl.ds(n0, lanes)]
                halves.append(acc)
            block = jnp.concatenate(halves, axis=0).astype(o_ref.dtype)
            o_ref[0, 0, pl.ds(16 * pair, 16), pl.ds(n0, lanes)] = block
        return carry

    lax.fori_loop(0, xs_ref.shape[1] // lanes, lane_body, 0)


def polyphase(in_block, fir_taps, spectra):
    tap_count, points = fir_taps.shape
    components, inputs_here = in_block.shape[0], in_block.shape[1]
    frames = in_block.shape[2] // points
    framed = in_block.reshape(components, inputs_here, frames, points)
    return pl.pallas_call(
        fir_kernel,
        grid=(components * inputs_here,),
        in_specs=[
            pl.BlockSpec(
                (1, 1, frames, points), lambda r: (r // inputs_here, r % inputs_here, 0, 0)
            ),
            pl.BlockSpec((tap_count, points), lambda r: (0, 0)),
        ],
        out_specs=pl.BlockSpec(
            (1, 1, spectra, points), lambda r: (r // inputs_here, r % inputs_here, 0, 0)
        ),
        out_shape=jax.ShapeDtypeStruct((components, inputs_here, spectra, points), jnp.bfloat16),
        scratch_shapes=[pltpu.VMEM((8 * pl.cdiv(frames, 8), points), jnp.float32)],
    )(framed, fir_taps)


def contract(left_rows, right_rows):
    contract_dims = (((1,), (1,)), ((), ()))
    return lax.dot_general(left_rows, right_rows, contract_dims, preferred_element_type=jnp.float32)


def spectrum(filtered, cos_table, sin_table, slot_gain):
    inputs_here, spectra, points = (filtered.shape[1], filtered.shape[2], filtered.shape[3])
    rows = inputs_here * spectra
    slots = cos_table.shape[0]
    tables = jnp.concatenate([cos_table, sin_table], axis=0)
    products = contract(tables, filtered.reshape(2 * rows, points))
    cos_re, cos_im = products[:slots, :rows], products[:slots, rows:]
    sin_re, sin_im = products[slots:, :rows], products[slots:, rows:]
    spec_re = cos_re + sin_im
    spec_im = cos_im - sin_re
    combined = jnp.concatenate(
        [spec_re.reshape(-1, inputs_here, spectra), spec_im.reshape(-1, inputs_here, spectra)],
        axis=2,
    )
    return (combined * slot_gain[:, None, None]).astype(jnp.bfloat16)


def form_beams(beam_data, weight_re, weight_im):
    spectra = beam_data.shape[2] // 2
    samples = beam_data.reshape(beam_data.shape[0], -1, 2, beam_data.shape[2])
    with_re = jnp.einsum("bs,jspt->jbpt", weight_re, samples, preferred_element_type=jnp.float32)
    with_im = jnp.einsum("bs,jspt->jbpt", weight_im, samples, preferred_element_type=jnp.float32)
    out_re = with_re[..., :spectra] - with_im[..., spectra:]
    out_im = with_re[..., spectra:] + with_im[..., :spectra]
    return jnp.concatenate([out_re, out_im], axis=3)


def per_device(
    voltages, fir_taps, cor_channels, beam_channels, cor_gain, beam_gain, beam_stations, beam_codes
):
    tap_count, points = fir_taps.shape
    stn_count = lax.axis_size(STN_AXES)
    sec_count = lax.axis_size("x")
    device_count = stn_count * sec_count
    inputs_here = voltages.shape[1]
    spectra = voltages.shape[2] // points - tap_count + 1
    filtered = polyphase(voltages, fir_taps, spectra)
    channel_of = jnp.concatenate([cor_channels, beam_channels])
    slot_gain = jnp.concatenate([cor_gain, beam_gain])
    cos_table, sin_table = lax.optimization_barrier(make_tables(channel_of, points))
    weight_re, weight_im = make_weights(beam_stations, beam_codes, STATIONS)
    spectra_all = spectrum(filtered, cos_table, sin_table, slot_gain)
    outgoing = spectra_all.reshape(2, stn_count, sec_count, 1, 1, inputs_here, 2 * spectra)
    turned = lax.all_to_all(
        lax.all_to_all(outgoing, STN_AXES, split_axis=1, concat_axis=3, tiled=True),
        "x",
        split_axis=2,
        concat_axis=4,
        tiled=True,
    )
    received = turned.reshape(2, device_count * inputs_here, 2 * spectra)
    cor_data = received[0]
    beam_data = received[1:2]
    swapped = jnp.concatenate([cor_data[:, spectra:], -cor_data[:, :spectra]], axis=1)
    vis_re = contract(cor_data, cor_data) / spectra
    vis_im = contract(swapped, cor_data) / spectra
    visibilities = jnp.stack([vis_re, vis_im])[None].astype(jnp.bfloat16)
    raw_beams = form_beams(beam_data, weight_re, weight_im)
    local_power = jnp.sum(raw_beams * raw_beams, axis=(0, 2, 3))
    summed_power = local_power
    for axis in PHYSICAL_AXES:
        summed_power = lax.psum(summed_power, axis)
    beam_power = summed_power / (device_count * raw_beams.shape[2] * raw_beams.shape[3])
    beams = (raw_beams * lax.rsqrt(beam_power + epsilon)[None, :, None, None]).astype(jnp.bfloat16)
    return (visibilities, beams)


def solution(mesh):
    stn_count, sec_count = mesh.devices.shape
    cores = 2
    y_count = 4
    z_count = stn_count // (y_count * cores)
    devices = mesh.devices.reshape(y_count, z_count, cores, sec_count)
    fine = jax.sharding.Mesh(devices, ("y", "z", "core", "x"))
    spread = ("y", "z", "core", "x")
    in_specs = (P(None, spread, None), P(), P(), P(), P(), P(), P(), P())
    out_specs = (P(spread, None, None, None), P(spread, None, None, None))
    return jax.shard_map(
        per_device, mesh=fine, in_specs=in_specs, out_specs=out_specs, check_vma=False
    )
```

```python
import math

import jax
import jax.numpy as jnp
from jax import lax
from jax.experimental import pallas as pl
from jax.experimental.pallas import tpu as pltpu
from jax.sharding import PartitionSpec as P

STATIONS = 512


epsilon = 1e-05

STN_AXES = ("y", "z", "core")
PHYSICAL_AXES = ("core", "x", "y", "z")
ALL_AXES = ("y", "z", "core", "x")


def make_tables(channel_of, points):
    outer = 64
    inner = points // outer
    step = 2.0 * math.pi / points
    a_index = jnp.arange(inner, dtype=jnp.int32)
    b_index = jnp.arange(outer, dtype=jnp.int32)
    a_turns = (channel_of[:, None] * a_index[None, :] % inner) * outer
    b_turns = channel_of[:, None] * b_index[None, :] % points
    a_angle = a_turns.astype(jnp.float32) * step
    b_angle = b_turns.astype(jnp.float32) * step
    ca, sa = jnp.cos(a_angle)[:, :, None], jnp.sin(a_angle)[:, :, None]
    cb, sb = jnp.cos(b_angle)[:, None, :], jnp.sin(b_angle)[:, None, :]
    table_scale = 1.0 / math.sqrt(points)
    cos_table = ((ca * cb - sa * sb) * table_scale).astype(jnp.bfloat16)
    sin_table = ((sa * cb + ca * sb) * table_scale).astype(jnp.bfloat16)
    slots = channel_of.shape[0]
    return (cos_table.reshape(slots, points), sin_table.reshape(slots, points))


def make_weights(beam_stations, beam_codes, stations):
    station_ids = jnp.arange(stations, dtype=jnp.int32)
    onehot = (beam_stations[:, :, None] == station_ids[None, None, :]).astype(jnp.float32)
    amplitude = (1 + beam_codes // 64).astype(jnp.float32)
    phase_angle = (beam_codes % 64).astype(jnp.float32) * (2.0 * math.pi / 64.0)
    weight_re = jnp.einsum("bk,bks->bs", amplitude * jnp.cos(phase_angle), onehot)
    weight_im = jnp.einsum("bk,bks->bs", amplitude * jnp.sin(phase_angle), onehot)
    return (weight_re.astype(jnp.bfloat16), weight_im.astype(jnp.bfloat16))


def fir_kernel(x_ref, h_ref, o_ref, xs_ref):
    tap_count = h_ref.shape[0]
    frames = x_ref.shape[2]
    spectra = o_ref.shape[2]
    lanes = 256
    xs_ref[pl.ds(0, frames), :] = x_ref[0, 0].astype(jnp.float32)

    def lane_body(lane_block, carry):
        n0 = pl.multiple_of(lane_block * lanes, lanes)
        taps = [
            jnp.broadcast_to(h_ref[pl.ds(t, 1), pl.ds(n0, lanes)], (8, lanes))
            for t in range(tap_count)
        ]
        for pair in range(spectra // 16):
            halves = []
            for half in range(2):
                s0 = 16 * pair + 8 * half
                acc = taps[0] * xs_ref[pl.ds(s0, 8), pl.ds(n0, lanes)]
                for t in range(1, tap_count):
                    acc = acc + taps[t] * xs_ref[pl.ds(s0 + t, 8), pl.ds(n0, lanes)]
                halves.append(acc)
            block = jnp.concatenate(halves, axis=0).astype(o_ref.dtype)
            o_ref[0, 0, pl.ds(16 * pair, 16), pl.ds(n0, lanes)] = block
        return carry

    lax.fori_loop(0, xs_ref.shape[1] // lanes, lane_body, 0)


def polyphase(in_block, fir_taps, spectra):
    tap_count, points = fir_taps.shape
    components, inputs_here = in_block.shape[0], in_block.shape[1]
    frames = in_block.shape[2] // points
    framed = in_block.reshape(components, inputs_here, frames, points)
    return pl.pallas_call(
        fir_kernel,
        grid=(components * inputs_here,),
        in_specs=[
            pl.BlockSpec(
                (1, 1, frames, points), lambda r: (r // inputs_here, r % inputs_here, 0, 0)
            ),
            pl.BlockSpec((tap_count, points), lambda r: (0, 0)),
        ],
        out_specs=pl.BlockSpec(
            (1, 1, spectra, points), lambda r: (r // inputs_here, r % inputs_here, 0, 0)
        ),
        out_shape=jax.ShapeDtypeStruct((components, inputs_here, spectra, points), jnp.bfloat16),
        scratch_shapes=[pltpu.VMEM((8 * pl.cdiv(frames, 8), points), jnp.float32)],
    )(framed, fir_taps)


def contract(left_rows, right_rows):
    contract_dims = (((1,), (1,)), ((), ()))
    return lax.dot_general(left_rows, right_rows, contract_dims, preferred_element_type=jnp.float32)


def spectrum(filtered, cos_table, sin_table, slot_gain):
    inputs_here, spectra, points = (filtered.shape[1], filtered.shape[2], filtered.shape[3])
    rows = inputs_here * spectra
    slots = cos_table.shape[0]
    tables = jnp.concatenate([cos_table, sin_table], axis=0)
    products = contract(tables, filtered.reshape(2 * rows, points))
    cos_re, cos_im = products[:slots, :rows], products[:slots, rows:]
    sin_re, sin_im = products[slots:, :rows], products[slots:, rows:]
    spec_re = cos_re + sin_im
    spec_im = cos_im - sin_re
    combined = jnp.concatenate(
        [spec_re.reshape(-1, inputs_here, spectra), spec_im.reshape(-1, inputs_here, spectra)],
        axis=2,
    )
    return (combined * slot_gain[:, None, None]).astype(jnp.bfloat16)


def form_beams(beam_data, weight_re, weight_im):
    spectra = beam_data.shape[2] // 2
    samples = beam_data.reshape(beam_data.shape[0], -1, 2, beam_data.shape[2])
    with_re = jnp.einsum("bs,jspt->jbpt", weight_re, samples, preferred_element_type=jnp.float32)
    with_im = jnp.einsum("bs,jspt->jbpt", weight_im, samples, preferred_element_type=jnp.float32)
    out_re = with_re[..., :spectra] - with_im[..., spectra:]
    out_im = with_re[..., spectra:] + with_im[..., :spectra]
    return jnp.concatenate([out_re, out_im], axis=3)


def per_device(
    voltages, fir_taps, cor_channels, beam_channels, cor_gain, beam_gain, beam_stations, beam_codes
):
    tap_count, points = fir_taps.shape
    stn_count = lax.axis_size(STN_AXES)
    sec_count = lax.axis_size("x")
    device_count = stn_count * sec_count
    inputs_here = voltages.shape[1]
    spectra = voltages.shape[2] // points - tap_count + 1
    filtered = polyphase(voltages, fir_taps, spectra)
    channel_of = jnp.concatenate([cor_channels, beam_channels])
    slot_gain = jnp.concatenate([cor_gain, beam_gain])
    cos_table, sin_table = lax.optimization_barrier(make_tables(channel_of, points))
    weight_re, weight_im = make_weights(beam_stations, beam_codes, STATIONS)
    spectra_all = spectrum(filtered, cos_table, sin_table, slot_gain)
    outgoing = spectra_all.reshape(2, device_count, inputs_here, 2 * spectra)
    turned = lax.all_to_all(outgoing, ALL_AXES, split_axis=1, concat_axis=1, tiled=True)
    received = turned.reshape(2, device_count * inputs_here, 2 * spectra)
    cor_data = received[0]
    beam_data = received[1:2]
    swapped = jnp.concatenate([cor_data[:, spectra:], -cor_data[:, :spectra]], axis=1)
    vis_re = contract(cor_data, cor_data) / spectra
    vis_im = contract(swapped, cor_data) / spectra
    visibilities = jnp.stack([vis_re, vis_im])[None].astype(jnp.bfloat16)
    raw_beams = form_beams(beam_data, weight_re, weight_im)
    local_power = jnp.sum(raw_beams * raw_beams, axis=(0, 2, 3))
    summed_power = local_power
    for axis in PHYSICAL_AXES:
        summed_power = lax.psum(summed_power, axis)
    beam_power = summed_power / (device_count * raw_beams.shape[2] * raw_beams.shape[3])
    beams = (raw_beams * lax.rsqrt(beam_power + epsilon)[None, :, None, None]).astype(jnp.bfloat16)
    return (visibilities, beams)


def solution(mesh):
    stn_count, sec_count = mesh.devices.shape
    cores = 2
    y_count = 4
    z_count = stn_count // (y_count * cores)
    devices = mesh.devices.reshape(y_count, z_count, cores, sec_count)
    fine = jax.sharding.Mesh(devices, ("y", "z", "core", "x"))
    spread = ("y", "z", "core", "x")
    in_specs = (P(None, spread, None), P(), P(), P(), P(), P(), P(), P())
    out_specs = (P(spread, None, None, None), P(spread, None, None, None))
    return jax.shard_map(
        per_device, mesh=fine, in_specs=in_specs, out_specs=out_specs, check_vma=False
    )
```

```python
import math

import jax
import jax.numpy as jnp
from jax import lax
from jax.experimental import pallas as pl
from jax.experimental.pallas import tpu as pltpu
from jax.sharding import PartitionSpec as P

STATIONS = 512


epsilon = 1e-05

STN_AXES = ("y", "z", "core")
PHYSICAL_AXES = ("core", "x", "y", "z")
ALL_AXES = ("y", "z", "core", "x")


def make_tables(channel_of, points):
    outer = 64
    inner = points // outer
    step = 2.0 * math.pi / points
    a_index = jnp.arange(inner, dtype=jnp.int32)
    b_index = jnp.arange(outer, dtype=jnp.int32)
    a_turns = (channel_of[:, None] * a_index[None, :] % inner) * outer
    b_turns = channel_of[:, None] * b_index[None, :] % points
    a_angle = a_turns.astype(jnp.float32) * step
    b_angle = b_turns.astype(jnp.float32) * step
    ca, sa = jnp.cos(a_angle)[:, :, None], jnp.sin(a_angle)[:, :, None]
    cb, sb = jnp.cos(b_angle)[:, None, :], jnp.sin(b_angle)[:, None, :]
    table_scale = 1.0 / math.sqrt(points)
    cos_table = ((ca * cb - sa * sb) * table_scale).astype(jnp.bfloat16)
    sin_table = ((sa * cb + ca * sb) * table_scale).astype(jnp.bfloat16)
    slots = channel_of.shape[0]
    return (cos_table.reshape(slots, points), sin_table.reshape(slots, points))


def make_weights(beam_stations, beam_codes, stations):
    station_ids = jnp.arange(stations, dtype=jnp.int32)
    onehot = (beam_stations[:, :, None] == station_ids[None, None, :]).astype(jnp.float32)
    amplitude = (1 + beam_codes // 64).astype(jnp.float32)
    phase_angle = (beam_codes % 64).astype(jnp.float32) * (2.0 * math.pi / 64.0)
    weight_re = jnp.einsum("bk,bks->bs", amplitude * jnp.cos(phase_angle), onehot)
    weight_im = jnp.einsum("bk,bks->bs", amplitude * jnp.sin(phase_angle), onehot)
    return (weight_re.astype(jnp.bfloat16), weight_im.astype(jnp.bfloat16))


def fir_kernel(x_ref, h_ref, o_ref, xs_ref):
    tap_count = h_ref.shape[0]
    frames = x_ref.shape[2]
    spectra = o_ref.shape[2]
    lanes = 256
    xs_ref[pl.ds(0, frames), :] = x_ref[0, 0].astype(jnp.float32)

    def lane_body(lane_block, carry):
        n0 = pl.multiple_of(lane_block * lanes, lanes)
        taps = [
            jnp.broadcast_to(h_ref[pl.ds(t, 1), pl.ds(n0, lanes)], (8, lanes))
            for t in range(tap_count)
        ]
        for pair in range(spectra // 16):
            halves = []
            for half in range(2):
                s0 = 16 * pair + 8 * half
                acc = taps[0] * xs_ref[pl.ds(s0, 8), pl.ds(n0, lanes)]
                for t in range(1, tap_count):
                    acc = acc + taps[t] * xs_ref[pl.ds(s0 + t, 8), pl.ds(n0, lanes)]
                halves.append(acc)
            block = jnp.concatenate(halves, axis=0).astype(o_ref.dtype)
            o_ref[0, 0, pl.ds(16 * pair, 16), pl.ds(n0, lanes)] = block
        return carry

    lax.fori_loop(0, xs_ref.shape[1] // lanes, lane_body, 0)


def polyphase(in_block, fir_taps, spectra):
    tap_count, points = fir_taps.shape
    components, inputs_here = in_block.shape[0], in_block.shape[1]
    frames = in_block.shape[2] // points
    framed = in_block.reshape(components, inputs_here, frames, points)
    return pl.pallas_call(
        fir_kernel,
        grid=(components * inputs_here,),
        in_specs=[
            pl.BlockSpec(
                (1, 1, frames, points), lambda r: (r // inputs_here, r % inputs_here, 0, 0)
            ),
            pl.BlockSpec((tap_count, points), lambda r: (0, 0)),
        ],
        out_specs=pl.BlockSpec(
            (1, 1, spectra, points), lambda r: (r // inputs_here, r % inputs_here, 0, 0)
        ),
        out_shape=jax.ShapeDtypeStruct((components, inputs_here, spectra, points), jnp.bfloat16),
        scratch_shapes=[pltpu.VMEM((8 * pl.cdiv(frames, 8), points), jnp.float32)],
    )(framed, fir_taps)


def contract(left_rows, right_rows):
    contract_dims = (((1,), (1,)), ((), ()))
    return lax.dot_general(left_rows, right_rows, contract_dims, preferred_element_type=jnp.float32)


def spectrum(filtered, cos_table, sin_table, slot_gain):
    inputs_here, spectra, points = (filtered.shape[1], filtered.shape[2], filtered.shape[3])
    rows = inputs_here * spectra
    slots = cos_table.shape[0]
    tables = jnp.concatenate([cos_table, sin_table], axis=0)
    products = contract(tables, filtered.reshape(2 * rows, points))
    cos_re, cos_im = products[:slots, :rows], products[:slots, rows:]
    sin_re, sin_im = products[slots:, :rows], products[slots:, rows:]
    spec_re = cos_re + sin_im
    spec_im = cos_im - sin_re
    combined = jnp.concatenate(
        [spec_re.reshape(-1, inputs_here, spectra), spec_im.reshape(-1, inputs_here, spectra)],
        axis=2,
    )
    return (combined * slot_gain[:, None, None]).astype(jnp.bfloat16)


def form_beams(beam_data, weight_re, weight_im):
    spectra = beam_data.shape[2] // 2
    samples = beam_data.reshape(beam_data.shape[0], -1, 2, beam_data.shape[2])
    with_re = jnp.einsum("bs,jspt->jbpt", weight_re, samples, preferred_element_type=jnp.float32)
    with_im = jnp.einsum("bs,jspt->jbpt", weight_im, samples, preferred_element_type=jnp.float32)
    out_re = with_re[..., :spectra] - with_im[..., spectra:]
    out_im = with_re[..., spectra:] + with_im[..., :spectra]
    return jnp.concatenate([out_re, out_im], axis=3)


def per_device(
    voltages, fir_taps, cor_channels, beam_channels, cor_gain, beam_gain, beam_stations, beam_codes
):
    tap_count, points = fir_taps.shape
    stn_count = lax.axis_size(STN_AXES)
    sec_count = lax.axis_size("x")
    device_count = stn_count * sec_count
    inputs_here = voltages.shape[1]
    spectra = voltages.shape[2] // points - tap_count + 1
    filtered = polyphase(voltages, fir_taps, spectra)
    channel_of = jnp.concatenate([cor_channels, beam_channels])
    slot_gain = jnp.concatenate([cor_gain, beam_gain])
    cos_table, sin_table = lax.optimization_barrier(make_tables(channel_of, points))
    weight_re, weight_im = make_weights(beam_stations, beam_codes, STATIONS)
    spectra_all = spectrum(filtered, cos_table, sin_table, slot_gain)
    outgoing = spectra_all.reshape(2, device_count, inputs_here, 2 * spectra)
    turned = lax.all_to_all(outgoing, ALL_AXES, split_axis=1, concat_axis=1, tiled=True)
    received = turned.reshape(2, device_count * inputs_here, 2 * spectra)
    cor_data = received[0]
    beam_data = received[1:2]
    swapped = jnp.concatenate([cor_data[:, spectra:], -cor_data[:, :spectra]], axis=1)
    vis_re = contract(cor_data, cor_data) / spectra
    vis_im = contract(swapped, cor_data) / spectra
    visibilities = jnp.stack([vis_re, vis_im])[None].astype(jnp.bfloat16)
    raw_beams = form_beams(beam_data, weight_re, weight_im)
    local_power = jnp.sum(raw_beams * raw_beams, axis=(0, 2, 3))
    spread_power = jnp.broadcast_to(local_power[None], (device_count, local_power.shape[0]))
    gathered_power = lax.all_to_all(spread_power, ALL_AXES, split_axis=0, concat_axis=0, tiled=True)
    summed_power = jnp.sum(gathered_power, axis=0)
    beam_power = summed_power / (device_count * raw_beams.shape[2] * raw_beams.shape[3])
    beams = (raw_beams * lax.rsqrt(beam_power + epsilon)[None, :, None, None]).astype(jnp.bfloat16)
    return (visibilities, beams)


def solution(mesh):
    stn_count, sec_count = mesh.devices.shape
    cores = 2
    y_count = 4
    z_count = stn_count // (y_count * cores)
    devices = mesh.devices.reshape(y_count, z_count, cores, sec_count)
    fine = jax.sharding.Mesh(devices, ("y", "z", "core", "x"))
    spread = ("y", "z", "core", "x")
    in_specs = (P(None, spread, None), P(), P(), P(), P(), P(), P(), P())
    out_specs = (P(spread, None, None, None), P(spread, None, None, None))
    return jax.shard_map(
        per_device, mesh=fine, in_specs=in_specs, out_specs=out_specs, check_vma=False
    )
```

```python
import math

import jax
import jax.numpy as jnp
from jax import lax
from jax.experimental import pallas as pl
from jax.experimental.pallas import tpu as pltpu
from jax.sharding import PartitionSpec as P

STATIONS = 512


epsilon = 1e-05

STN_AXES = ("y", "z", "core")
PHYSICAL_AXES = ("core", "x", "y", "z")
ALL_AXES = ("y", "z", "core", "x")


def make_tables(channel_of, points):
    outer = 64
    inner = points // outer
    step = 2.0 * math.pi / points
    a_index = jnp.arange(inner, dtype=jnp.int32)
    b_index = jnp.arange(outer, dtype=jnp.int32)
    a_turns = (channel_of[:, None] * a_index[None, :] % inner) * outer
    b_turns = channel_of[:, None] * b_index[None, :] % points
    a_angle = a_turns.astype(jnp.float32) * step
    b_angle = b_turns.astype(jnp.float32) * step
    ca, sa = jnp.cos(a_angle)[:, :, None], jnp.sin(a_angle)[:, :, None]
    cb, sb = jnp.cos(b_angle)[:, None, :], jnp.sin(b_angle)[:, None, :]
    table_scale = 1.0 / math.sqrt(points)
    cos_table = ((ca * cb - sa * sb) * table_scale).astype(jnp.bfloat16)
    sin_table = ((sa * cb + ca * sb) * table_scale).astype(jnp.bfloat16)
    slots = channel_of.shape[0]
    return (cos_table.reshape(slots, points), sin_table.reshape(slots, points))


def make_weights(beam_stations, beam_codes, stations):
    station_ids = jnp.arange(stations, dtype=jnp.int32)
    onehot = (beam_stations[:, :, None] == station_ids[None, None, :]).astype(jnp.float32)
    amplitude = (1 + beam_codes // 64).astype(jnp.float32)
    phase_angle = (beam_codes % 64).astype(jnp.float32) * (2.0 * math.pi / 64.0)
    weight_re = jnp.einsum("bk,bks->bs", amplitude * jnp.cos(phase_angle), onehot)
    weight_im = jnp.einsum("bk,bks->bs", amplitude * jnp.sin(phase_angle), onehot)
    return (weight_re.astype(jnp.bfloat16), weight_im.astype(jnp.bfloat16))


def fir_kernel(x_ref, h_ref, o_ref, xs_ref, os_ref):
    tap_count = h_ref.shape[0]
    frames = x_ref.shape[2]
    spectra = o_ref.shape[2]
    stride = 16
    depth = spectra // stride
    lanes = 128

    def lane_body(lane_block, carry):
        n0 = pl.multiple_of(lane_block * lanes, lanes)
        xs_ref[pl.ds(0, frames), :] = x_ref[0, 0, :, pl.ds(n0, lanes)].astype(jnp.float32)
        groups = [
            xs_ref[pl.ds(g, depth, stride=stride), :] for g in range(stride + tap_count - 1)
        ]
        taps = [
            jnp.broadcast_to(h_ref[pl.ds(t, 1), pl.ds(n0, lanes)], (depth, lanes))
            for t in range(tap_count)
        ]
        for q in range(stride):
            acc = taps[0] * groups[q]
            for t in range(1, tap_count):
                acc = acc + taps[t] * groups[q + t]
            os_ref[pl.ds(q, depth, stride=stride), :] = acc
        o_ref[0, 0, :, pl.ds(n0, lanes)] = os_ref[...].astype(o_ref.dtype)
        return carry

    lax.fori_loop(0, h_ref.shape[1] // lanes, lane_body, 0)


def polyphase(in_block, fir_taps, spectra):
    tap_count, points = fir_taps.shape
    components, inputs_here = in_block.shape[0], in_block.shape[1]
    frames = in_block.shape[2] // points
    framed = in_block.reshape(components, inputs_here, frames, points)
    return pl.pallas_call(
        fir_kernel,
        grid=(components * inputs_here,),
        in_specs=[
            pl.BlockSpec(
                (1, 1, frames, points), lambda r: (r // inputs_here, r % inputs_here, 0, 0)
            ),
            pl.BlockSpec((tap_count, points), lambda r: (0, 0)),
        ],
        out_specs=pl.BlockSpec(
            (1, 1, spectra, points), lambda r: (r // inputs_here, r % inputs_here, 0, 0)
        ),
        out_shape=jax.ShapeDtypeStruct((components, inputs_here, spectra, points), jnp.bfloat16),
        scratch_shapes=[
            pltpu.VMEM((8 * pl.cdiv(frames, 8), 128), jnp.float32),
            pltpu.VMEM((spectra, 128), jnp.float32),
        ],
    )(framed, fir_taps)


def contract(left_rows, right_rows):
    contract_dims = (((1,), (1,)), ((), ()))
    return lax.dot_general(left_rows, right_rows, contract_dims, preferred_element_type=jnp.float32)


def spectrum(filtered, cos_table, sin_table, slot_gain):
    inputs_here, spectra, points = (filtered.shape[1], filtered.shape[2], filtered.shape[3])
    rows = inputs_here * spectra
    slots = cos_table.shape[0]
    tables = jnp.concatenate([cos_table, sin_table], axis=0)
    products = contract(tables, filtered.reshape(2 * rows, points))
    cos_re, cos_im = products[:slots, :rows], products[:slots, rows:]
    sin_re, sin_im = products[slots:, :rows], products[slots:, rows:]
    spec_re = cos_re + sin_im
    spec_im = cos_im - sin_re
    combined = jnp.concatenate(
        [spec_re.reshape(-1, inputs_here, spectra), spec_im.reshape(-1, inputs_here, spectra)],
        axis=2,
    )
    return (combined * slot_gain[:, None, None]).astype(jnp.bfloat16)


def form_beams(beam_data, weight_re, weight_im):
    spectra = beam_data.shape[2] // 2
    samples = beam_data.reshape(beam_data.shape[0], -1, 2, beam_data.shape[2])
    with_re = jnp.einsum("bs,jspt->jbpt", weight_re, samples, preferred_element_type=jnp.float32)
    with_im = jnp.einsum("bs,jspt->jbpt", weight_im, samples, preferred_element_type=jnp.float32)
    out_re = with_re[..., :spectra] - with_im[..., spectra:]
    out_im = with_re[..., spectra:] + with_im[..., :spectra]
    return jnp.concatenate([out_re, out_im], axis=3)


def per_device(
    voltages, fir_taps, cor_channels, beam_channels, cor_gain, beam_gain, beam_stations, beam_codes
):
    tap_count, points = fir_taps.shape
    stn_count = lax.axis_size(STN_AXES)
    sec_count = lax.axis_size("x")
    device_count = stn_count * sec_count
    inputs_here = voltages.shape[1]
    spectra = voltages.shape[2] // points - tap_count + 1
    filtered = polyphase(voltages, fir_taps, spectra)
    channel_of = jnp.concatenate([cor_channels, beam_channels])
    slot_gain = jnp.concatenate([cor_gain, beam_gain])
    cos_table, sin_table = lax.optimization_barrier(make_tables(channel_of, points))
    weight_re, weight_im = make_weights(beam_stations, beam_codes, STATIONS)
    spectra_all = spectrum(filtered, cos_table, sin_table, slot_gain)
    outgoing = spectra_all.reshape(2, device_count, inputs_here, 2 * spectra)
    turned = lax.all_to_all(outgoing, ALL_AXES, split_axis=1, concat_axis=1, tiled=True)
    received = turned.reshape(2, device_count * inputs_here, 2 * spectra)
    cor_data = received[0]
    beam_data = received[1:2]
    swapped = jnp.concatenate([cor_data[:, spectra:], -cor_data[:, :spectra]], axis=1)
    vis_re = contract(cor_data, cor_data) / spectra
    vis_im = contract(swapped, cor_data) / spectra
    visibilities = jnp.stack([vis_re, vis_im])[None].astype(jnp.bfloat16)
    raw_beams = form_beams(beam_data, weight_re, weight_im)
    local_power = jnp.sum(raw_beams * raw_beams, axis=(0, 2, 3))
    spread_power = jnp.broadcast_to(local_power[None], (device_count, local_power.shape[0]))
    gathered_power = lax.all_to_all(spread_power, ALL_AXES, split_axis=0, concat_axis=0, tiled=True)
    summed_power = jnp.sum(gathered_power, axis=0)
    beam_power = summed_power / (device_count * raw_beams.shape[2] * raw_beams.shape[3])
    beams = (raw_beams * lax.rsqrt(beam_power + epsilon)[None, :, None, None]).astype(jnp.bfloat16)
    return (visibilities, beams)


def solution(mesh):
    stn_count, sec_count = mesh.devices.shape
    cores = 2
    y_count = 4
    z_count = stn_count // (y_count * cores)
    devices = mesh.devices.reshape(y_count, z_count, cores, sec_count)
    fine = jax.sharding.Mesh(devices, ("y", "z", "core", "x"))
    spread = ("y", "z", "core", "x")
    in_specs = (P(None, spread, None), P(), P(), P(), P(), P(), P(), P())
    out_specs = (P(spread, None, None, None), P(spread, None, None, None))
    return jax.shard_map(
        per_device, mesh=fine, in_specs=in_specs, out_specs=out_specs, check_vma=False
    )
```

```python
import math

import jax
import jax.numpy as jnp
from jax import lax
from jax.experimental import pallas as pl
from jax.experimental.pallas import tpu as pltpu
from jax.sharding import PartitionSpec as P

STATIONS = 512


epsilon = 1e-05

STN_AXES = ("y", "z", "core")
PHYSICAL_AXES = ("core", "x", "y", "z")
ALL_AXES = ("y", "z", "core", "x")


def make_tables(channel_of, points):
    outer = 64
    inner = points // outer
    step = 2.0 * math.pi / points
    a_index = jnp.arange(inner, dtype=jnp.int32)
    b_index = jnp.arange(outer, dtype=jnp.int32)
    a_turns = (channel_of[:, None] * a_index[None, :] % inner) * outer
    b_turns = channel_of[:, None] * b_index[None, :] % points
    a_angle = a_turns.astype(jnp.float32) * step
    b_angle = b_turns.astype(jnp.float32) * step
    ca, sa = jnp.cos(a_angle)[:, :, None], jnp.sin(a_angle)[:, :, None]
    cb, sb = jnp.cos(b_angle)[:, None, :], jnp.sin(b_angle)[:, None, :]
    table_scale = 1.0 / math.sqrt(points)
    cos_table = ((ca * cb - sa * sb) * table_scale).astype(jnp.bfloat16)
    sin_table = ((sa * cb + ca * sb) * table_scale).astype(jnp.bfloat16)
    slots = channel_of.shape[0]
    return (cos_table.reshape(slots, points), sin_table.reshape(slots, points))


def make_weights(beam_stations, beam_codes, stations):
    station_ids = jnp.arange(stations, dtype=jnp.int32)
    onehot = (beam_stations[:, :, None] == station_ids[None, None, :]).astype(jnp.float32)
    amplitude = (1 + beam_codes // 64).astype(jnp.float32)
    phase_angle = (beam_codes % 64).astype(jnp.float32) * (2.0 * math.pi / 64.0)
    weight_re = jnp.einsum("bk,bks->bs", amplitude * jnp.cos(phase_angle), onehot)
    weight_im = jnp.einsum("bk,bks->bs", amplitude * jnp.sin(phase_angle), onehot)
    return (weight_re.astype(jnp.bfloat16), weight_im.astype(jnp.bfloat16))


def fir_kernel(x_ref, h_ref, o_ref, os_ref):
    tap_count, points = h_ref.shape
    inputs_here = o_ref.shape[1]
    spectra = o_ref.shape[2]
    stride = 16
    depth = spectra // stride
    lanes = 128
    frame_rows = points // lanes * inputs_here

    def lane_body(step, carry):
        input_index = step % inputs_here
        lane_block = step // inputs_here
        n0 = pl.multiple_of(lane_block * lanes, lanes)
        first = lane_block * inputs_here + input_index
        groups = [
            x_ref[0, pl.ds(first + g * frame_rows, depth, stride=stride * frame_rows), :]
            for g in range(stride + tap_count - 1)
        ]
        taps = [
            jnp.broadcast_to(h_ref[pl.ds(t, 1), pl.ds(n0, lanes)], (depth, lanes))
            for t in range(tap_count)
        ]
        for q in range(stride):
            acc = taps[0] * groups[q]
            for t in range(1, tap_count):
                acc = acc + taps[t] * groups[q + t]
            os_ref[pl.ds(q, depth, stride=stride), :] = acc
        o_ref[0, input_index, :, pl.ds(n0, lanes)] = os_ref[...].astype(o_ref.dtype)
        return carry

    lax.fori_loop(0, points // lanes * inputs_here, lane_body, 0)


def polyphase(in_block, fir_taps, spectra):
    tap_count, points = fir_taps.shape
    components, inputs_here, samples = in_block.shape
    lanes = 128
    rows = samples // lanes * inputs_here
    tiles = in_block.reshape(components, inputs_here, samples // lanes, lanes)
    tiles = jnp.transpose(tiles, (0, 2, 1, 3)).reshape(components, rows, lanes)
    tiles = tiles.astype(jnp.float32)
    return pl.pallas_call(
        fir_kernel,
        grid=(components,),
        in_specs=[
            pl.BlockSpec((1, rows, lanes), lambda c: (c, 0, 0)),
            pl.BlockSpec((tap_count, points), lambda c: (0, 0)),
        ],
        out_specs=pl.BlockSpec((1, inputs_here, spectra, points), lambda c: (c, 0, 0, 0)),
        out_shape=jax.ShapeDtypeStruct((components, inputs_here, spectra, points), jnp.bfloat16),
        scratch_shapes=[pltpu.VMEM((spectra, lanes), jnp.float32)],
    )(tiles, fir_taps)


def contract(left_rows, right_rows):
    contract_dims = (((1,), (1,)), ((), ()))
    return lax.dot_general(left_rows, right_rows, contract_dims, preferred_element_type=jnp.float32)


def spectrum(filtered, cos_table, sin_table, slot_gain):
    inputs_here, spectra, points = (filtered.shape[1], filtered.shape[2], filtered.shape[3])
    rows = inputs_here * spectra
    slots = cos_table.shape[0]
    tables = jnp.concatenate([cos_table, sin_table], axis=0)
    products = contract(tables, filtered.reshape(2 * rows, points))
    cos_re, cos_im = products[:slots, :rows], products[:slots, rows:]
    sin_re, sin_im = products[slots:, :rows], products[slots:, rows:]
    spec_re = cos_re + sin_im
    spec_im = cos_im - sin_re
    combined = jnp.concatenate(
        [spec_re.reshape(-1, inputs_here, spectra), spec_im.reshape(-1, inputs_here, spectra)],
        axis=2,
    )
    return (combined * slot_gain[:, None, None]).astype(jnp.bfloat16)


def form_beams(beam_data, weight_re, weight_im):
    spectra = beam_data.shape[2] // 2
    samples = beam_data.reshape(beam_data.shape[0], -1, 2, beam_data.shape[2])
    with_re = jnp.einsum("bs,jspt->jbpt", weight_re, samples, preferred_element_type=jnp.float32)
    with_im = jnp.einsum("bs,jspt->jbpt", weight_im, samples, preferred_element_type=jnp.float32)
    out_re = with_re[..., :spectra] - with_im[..., spectra:]
    out_im = with_re[..., spectra:] + with_im[..., :spectra]
    return jnp.concatenate([out_re, out_im], axis=3)


def per_device(
    voltages, fir_taps, cor_channels, beam_channels, cor_gain, beam_gain, beam_stations, beam_codes
):
    tap_count, points = fir_taps.shape
    stn_count = lax.axis_size(STN_AXES)
    sec_count = lax.axis_size("x")
    device_count = stn_count * sec_count
    inputs_here = voltages.shape[1]
    spectra = voltages.shape[2] // points - tap_count + 1
    filtered = polyphase(voltages, fir_taps, spectra)
    channel_of = jnp.concatenate([cor_channels, beam_channels])
    slot_gain = jnp.concatenate([cor_gain, beam_gain])
    cos_table, sin_table = lax.optimization_barrier(make_tables(channel_of, points))
    weight_re, weight_im = make_weights(beam_stations, beam_codes, STATIONS)
    spectra_all = spectrum(filtered, cos_table, sin_table, slot_gain)
    outgoing = spectra_all.reshape(2, device_count, inputs_here, 2 * spectra)
    turned = lax.all_to_all(outgoing, ALL_AXES, split_axis=1, concat_axis=1, tiled=True)
    received = turned.reshape(2, device_count * inputs_here, 2 * spectra)
    cor_data = received[0]
    beam_data = received[1:2]
    swapped = jnp.concatenate([cor_data[:, spectra:], -cor_data[:, :spectra]], axis=1)
    vis_re = contract(cor_data, cor_data) / spectra
    vis_im = contract(swapped, cor_data) / spectra
    visibilities = jnp.stack([vis_re, vis_im])[None].astype(jnp.bfloat16)
    raw_beams = form_beams(beam_data, weight_re, weight_im)
    local_power = jnp.sum(raw_beams * raw_beams, axis=(0, 2, 3))
    spread_power = jnp.broadcast_to(local_power[None], (device_count, local_power.shape[0]))
    gathered_power = lax.all_to_all(spread_power, ALL_AXES, split_axis=0, concat_axis=0, tiled=True)
    summed_power = jnp.sum(gathered_power, axis=0)
    beam_power = summed_power / (device_count * raw_beams.shape[2] * raw_beams.shape[3])
    beams = (raw_beams * lax.rsqrt(beam_power + epsilon)[None, :, None, None]).astype(jnp.bfloat16)
    return (visibilities, beams)


def solution(mesh):
    stn_count, sec_count = mesh.devices.shape
    cores = 2
    y_count = 4
    z_count = stn_count // (y_count * cores)
    devices = mesh.devices.reshape(y_count, z_count, cores, sec_count)
    fine = jax.sharding.Mesh(devices, ("y", "z", "core", "x"))
    spread = ("y", "z", "core", "x")
    in_specs = (P(None, spread, None), P(), P(), P(), P(), P(), P(), P())
    out_specs = (P(spread, None, None, None), P(spread, None, None, None))
    return jax.shard_map(
        per_device, mesh=fine, in_specs=in_specs, out_specs=out_specs, check_vma=False
    )
```

```python
import math

import jax
import jax.numpy as jnp
from jax import lax
from jax.experimental import pallas as pl
from jax.experimental.pallas import tpu as pltpu
from jax.sharding import PartitionSpec as P

STATIONS = 512


epsilon = 1e-05

STN_AXES = ("y", "z", "core")
PHYSICAL_AXES = ("core", "x", "y", "z")
ALL_AXES = ("y", "z", "core", "x")


def make_tables(channel_of, points):
    outer = 64
    inner = points // outer
    step = 2.0 * math.pi / points
    a_index = jnp.arange(inner, dtype=jnp.int32)
    b_index = jnp.arange(outer, dtype=jnp.int32)
    a_turns = (channel_of[:, None] * a_index[None, :] % inner) * outer
    b_turns = channel_of[:, None] * b_index[None, :] % points
    a_angle = a_turns.astype(jnp.float32) * step
    b_angle = b_turns.astype(jnp.float32) * step
    ca, sa = jnp.cos(a_angle)[:, :, None], jnp.sin(a_angle)[:, :, None]
    cb, sb = jnp.cos(b_angle)[:, None, :], jnp.sin(b_angle)[:, None, :]
    table_scale = 1.0 / math.sqrt(points)
    cos_table = ((ca * cb - sa * sb) * table_scale).astype(jnp.bfloat16)
    sin_table = ((sa * cb + ca * sb) * table_scale).astype(jnp.bfloat16)
    slots = channel_of.shape[0]
    return (cos_table.reshape(slots, points), sin_table.reshape(slots, points))


def make_weights(beam_stations, beam_codes, stations):
    station_ids = jnp.arange(stations, dtype=jnp.int32)
    onehot = (beam_stations[:, :, None] == station_ids[None, None, :]).astype(jnp.float32)
    amplitude = (1 + beam_codes // 64).astype(jnp.float32)
    phase_angle = (beam_codes % 64).astype(jnp.float32) * (2.0 * math.pi / 64.0)
    weight_re = jnp.einsum("bk,bks->bs", amplitude * jnp.cos(phase_angle), onehot)
    weight_im = jnp.einsum("bk,bks->bs", amplitude * jnp.sin(phase_angle), onehot)
    return (weight_re.astype(jnp.bfloat16), weight_im.astype(jnp.bfloat16))


def fir_kernel(x_ref, h_ref, o_ref, os_ref):
    tap_count = h_ref.shape[0]
    blocks, rows, lanes = x_ref.shape[1], x_ref.shape[2], x_ref.shape[3]
    inputs_here = o_ref.shape[1]
    spectra = o_ref.shape[2]
    for block in range(blocks):
        taps = [
            jnp.broadcast_to(h_ref[pl.ds(t, 1), pl.ds(block * lanes, lanes)], (rows, lanes))
            for t in range(tap_count)
        ]

        def frame_body(s, carry):
            acc = taps[0] * x_ref[s, block]
            for t in range(1, tap_count):
                acc = acc + taps[t] * x_ref[s + t, block]
            os_ref[pl.ds(s, rows, stride=spectra), :] = acc
            return carry

        lax.fori_loop(0, spectra, frame_body, 0, unroll=8)
        for r in range(rows):
            o_ref[r // inputs_here, r % inputs_here, :, pl.ds(block * lanes, lanes)] = os_ref[
                pl.ds(r * spectra, spectra), :
            ].astype(o_ref.dtype)


def polyphase(in_block, fir_taps, spectra):
    tap_count, points = fir_taps.shape
    components, inputs_here, samples = in_block.shape
    rows = components * inputs_here
    lanes = 128
    frames = samples // points
    per_frame = points // lanes
    tiles = in_block.reshape(components, inputs_here, samples // lanes, lanes)
    tiles = jnp.transpose(tiles, (2, 0, 1, 3)).astype(jnp.float32)
    tiles = tiles.reshape(frames, per_frame, rows, lanes)
    blocks = 4
    return pl.pallas_call(
        fir_kernel,
        grid=(per_frame // blocks,),
        in_specs=[
            pl.BlockSpec((frames, blocks, rows, lanes), lambda b: (0, b, 0, 0)),
            pl.BlockSpec((tap_count, blocks * lanes), lambda b: (0, b)),
        ],
        out_specs=pl.BlockSpec(
            (components, inputs_here, spectra, blocks * lanes), lambda b: (0, 0, 0, b)
        ),
        out_shape=jax.ShapeDtypeStruct((components, inputs_here, spectra, points), jnp.bfloat16),
        scratch_shapes=[pltpu.VMEM((rows * spectra, lanes), jnp.float32)],
    )(tiles, fir_taps)


def contract(left_rows, right_rows):
    contract_dims = (((1,), (1,)), ((), ()))
    return lax.dot_general(left_rows, right_rows, contract_dims, preferred_element_type=jnp.float32)


def spectrum(filtered, cos_table, sin_table, slot_gain):
    inputs_here, spectra, points = (filtered.shape[1], filtered.shape[2], filtered.shape[3])
    rows = inputs_here * spectra
    slots = cos_table.shape[0]
    tables = jnp.concatenate([cos_table, sin_table], axis=0)
    products = contract(tables, filtered.reshape(2 * rows, points))
    cos_re, cos_im = products[:slots, :rows], products[:slots, rows:]
    sin_re, sin_im = products[slots:, :rows], products[slots:, rows:]
    spec_re = cos_re + sin_im
    spec_im = cos_im - sin_re
    combined = jnp.concatenate(
        [spec_re.reshape(-1, inputs_here, spectra), spec_im.reshape(-1, inputs_here, spectra)],
        axis=2,
    )
    return (combined * slot_gain[:, None, None]).astype(jnp.bfloat16)


def form_beams(beam_data, weight_re, weight_im):
    spectra = beam_data.shape[2] // 2
    samples = beam_data.reshape(beam_data.shape[0], -1, 2, beam_data.shape[2])
    with_re = jnp.einsum("bs,jspt->jbpt", weight_re, samples, preferred_element_type=jnp.float32)
    with_im = jnp.einsum("bs,jspt->jbpt", weight_im, samples, preferred_element_type=jnp.float32)
    out_re = with_re[..., :spectra] - with_im[..., spectra:]
    out_im = with_re[..., spectra:] + with_im[..., :spectra]
    return jnp.concatenate([out_re, out_im], axis=3)


def per_device(
    voltages, fir_taps, cor_channels, beam_channels, cor_gain, beam_gain, beam_stations, beam_codes
):
    tap_count, points = fir_taps.shape
    stn_count = lax.axis_size(STN_AXES)
    sec_count = lax.axis_size("x")
    device_count = stn_count * sec_count
    inputs_here = voltages.shape[1]
    spectra = voltages.shape[2] // points - tap_count + 1
    filtered = polyphase(voltages, fir_taps, spectra)
    channel_of = jnp.concatenate([cor_channels, beam_channels])
    slot_gain = jnp.concatenate([cor_gain, beam_gain])
    cos_table, sin_table = lax.optimization_barrier(make_tables(channel_of, points))
    weight_re, weight_im = make_weights(beam_stations, beam_codes, STATIONS)
    spectra_all = spectrum(filtered, cos_table, sin_table, slot_gain)
    outgoing = spectra_all.reshape(2, device_count, inputs_here, 2 * spectra)
    turned = lax.all_to_all(outgoing, ALL_AXES, split_axis=1, concat_axis=1, tiled=True)
    received = turned.reshape(2, device_count * inputs_here, 2 * spectra)
    cor_data = received[0]
    beam_data = received[1:2]
    swapped = jnp.concatenate([cor_data[:, spectra:], -cor_data[:, :spectra]], axis=1)
    vis_re = contract(cor_data, cor_data) / spectra
    vis_im = contract(swapped, cor_data) / spectra
    visibilities = jnp.stack([vis_re, vis_im])[None].astype(jnp.bfloat16)
    raw_beams = form_beams(beam_data, weight_re, weight_im)
    local_power = jnp.sum(raw_beams * raw_beams, axis=(0, 2, 3))
    spread_power = jnp.broadcast_to(local_power[None], (device_count, local_power.shape[0]))
    gathered_power = lax.all_to_all(spread_power, ALL_AXES, split_axis=0, concat_axis=0, tiled=True)
    summed_power = jnp.sum(gathered_power, axis=0)
    beam_power = summed_power / (device_count * raw_beams.shape[2] * raw_beams.shape[3])
    beams = (raw_beams * lax.rsqrt(beam_power + epsilon)[None, :, None, None]).astype(jnp.bfloat16)
    return (visibilities, beams)


def solution(mesh):
    stn_count, sec_count = mesh.devices.shape
    cores = 2
    y_count = 4
    z_count = stn_count // (y_count * cores)
    devices = mesh.devices.reshape(y_count, z_count, cores, sec_count)
    fine = jax.sharding.Mesh(devices, ("y", "z", "core", "x"))
    spread = ("y", "z", "core", "x")
    in_specs = (P(None, spread, None), P(), P(), P(), P(), P(), P(), P())
    out_specs = (P(spread, None, None, None), P(spread, None, None, None))
    return jax.shard_map(
        per_device, mesh=fine, in_specs=in_specs, out_specs=out_specs, check_vma=False
    )
```

```python
import math

import jax
import jax.numpy as jnp
from jax import lax
from jax.experimental import pallas as pl
from jax.experimental.pallas import tpu as pltpu
from jax.sharding import PartitionSpec as P

STATIONS = 512


epsilon = 1e-05

STN_AXES = ("y", "z", "core")
PHYSICAL_AXES = ("core", "x", "y", "z")
ALL_AXES = ("y", "z", "core", "x")
FRAME_GROUP = 8


def make_tables(channel_of, points):
    outer = 64
    inner = points // outer
    step = 2.0 * math.pi / points
    a_index = jnp.arange(inner, dtype=jnp.int32)
    b_index = jnp.arange(outer, dtype=jnp.int32)
    a_turns = (channel_of[:, None] * a_index[None, :] % inner) * outer
    b_turns = channel_of[:, None] * b_index[None, :] % points
    a_angle = a_turns.astype(jnp.float32) * step
    b_angle = b_turns.astype(jnp.float32) * step
    ca, sa = jnp.cos(a_angle)[:, :, None], jnp.sin(a_angle)[:, :, None]
    cb, sb = jnp.cos(b_angle)[:, None, :], jnp.sin(b_angle)[:, None, :]
    table_scale = 1.0 / math.sqrt(points)
    cos_table = ((ca * cb - sa * sb) * table_scale).astype(jnp.bfloat16)
    sin_table = ((sa * cb + ca * sb) * table_scale).astype(jnp.bfloat16)
    slots = channel_of.shape[0]
    return (cos_table.reshape(slots, points), sin_table.reshape(slots, points))


def make_weights(beam_stations, beam_codes, stations):
    station_ids = jnp.arange(stations, dtype=jnp.int32)
    onehot = (beam_stations[:, :, None] == station_ids[None, None, :]).astype(jnp.float32)
    amplitude = (1 + beam_codes // 64).astype(jnp.float32)
    phase_angle = (beam_codes % 64).astype(jnp.float32) * (2.0 * math.pi / 64.0)
    weight_re = jnp.einsum("bk,bks->bs", amplitude * jnp.cos(phase_angle), onehot)
    weight_im = jnp.einsum("bk,bks->bs", amplitude * jnp.sin(phase_angle), onehot)
    return (weight_re.astype(jnp.bfloat16), weight_im.astype(jnp.bfloat16))


def fir_kernel(x_ref, h_ref, o_ref, os_ref):
    tap_count = h_ref.shape[0]
    blocks, rows, lanes = x_ref.shape[1], x_ref.shape[2], x_ref.shape[3]
    inputs_here = o_ref.shape[1]
    spectra = o_ref.shape[2]
    for block in range(blocks):
        taps = [
            jnp.broadcast_to(h_ref[pl.ds(t, 1), pl.ds(block * lanes, lanes)], (rows, lanes))
            for t in range(tap_count)
        ]

        def frame_body(step, carry):
            first = pl.multiple_of(step * FRAME_GROUP, FRAME_GROUP)
            window = [x_ref[first + f, block] for f in range(FRAME_GROUP + tap_count - 1)]
            for k in range(FRAME_GROUP):
                acc = taps[0] * window[k]
                for t in range(1, tap_count):
                    acc = acc + taps[t] * window[k + t]
                os_ref[pl.ds(first + k, rows, stride=spectra), :] = acc
            return carry

        lax.fori_loop(0, spectra // FRAME_GROUP, frame_body, 0)
        for r in range(rows):
            o_ref[r // inputs_here, r % inputs_here, :, pl.ds(block * lanes, lanes)] = os_ref[
                pl.ds(r * spectra, spectra), :
            ].astype(o_ref.dtype)


def polyphase(in_block, fir_taps, spectra):
    tap_count, points = fir_taps.shape
    components, inputs_here, samples = in_block.shape
    rows = components * inputs_here
    lanes = 128
    frames = samples // points
    per_frame = points // lanes
    tiles = in_block.reshape(components, inputs_here, samples // lanes, lanes)
    tiles = jnp.transpose(tiles, (2, 0, 1, 3)).astype(jnp.float32)
    tiles = tiles.reshape(frames, per_frame, rows, lanes)
    blocks = 4
    return pl.pallas_call(
        fir_kernel,
        grid=(per_frame // blocks,),
        in_specs=[
            pl.BlockSpec((frames, blocks, rows, lanes), lambda b: (0, b, 0, 0)),
            pl.BlockSpec((tap_count, blocks * lanes), lambda b: (0, b)),
        ],
        out_specs=pl.BlockSpec(
            (components, inputs_here, spectra, blocks * lanes), lambda b: (0, 0, 0, b)
        ),
        out_shape=jax.ShapeDtypeStruct((components, inputs_here, spectra, points), jnp.bfloat16),
        scratch_shapes=[pltpu.VMEM((rows * spectra, lanes), jnp.float32)],
    )(tiles, fir_taps)


def contract(left_rows, right_rows):
    contract_dims = (((1,), (1,)), ((), ()))
    return lax.dot_general(left_rows, right_rows, contract_dims, preferred_element_type=jnp.float32)


def spectrum(filtered, cos_table, sin_table, slot_gain):
    inputs_here, spectra, points = (filtered.shape[1], filtered.shape[2], filtered.shape[3])
    rows = inputs_here * spectra
    slots = cos_table.shape[0]
    tables = jnp.concatenate([cos_table, sin_table], axis=0)
    products = contract(tables, filtered.reshape(2 * rows, points))
    cos_re, cos_im = products[:slots, :rows], products[:slots, rows:]
    sin_re, sin_im = products[slots:, :rows], products[slots:, rows:]
    spec_re = cos_re + sin_im
    spec_im = cos_im - sin_re
    combined = jnp.concatenate(
        [spec_re.reshape(-1, inputs_here, spectra), spec_im.reshape(-1, inputs_here, spectra)],
        axis=2,
    )
    return (combined * slot_gain[:, None, None]).astype(jnp.bfloat16)


def form_beams(beam_data, weight_re, weight_im):
    spectra = beam_data.shape[2] // 2
    samples = beam_data.reshape(beam_data.shape[0], -1, 2, beam_data.shape[2])
    with_re = jnp.einsum("bs,jspt->jbpt", weight_re, samples, preferred_element_type=jnp.float32)
    with_im = jnp.einsum("bs,jspt->jbpt", weight_im, samples, preferred_element_type=jnp.float32)
    out_re = with_re[..., :spectra] - with_im[..., spectra:]
    out_im = with_re[..., spectra:] + with_im[..., :spectra]
    return jnp.concatenate([out_re, out_im], axis=3)


def per_device(
    voltages, fir_taps, cor_channels, beam_channels, cor_gain, beam_gain, beam_stations, beam_codes
):
    tap_count, points = fir_taps.shape
    stn_count = lax.axis_size(STN_AXES)
    sec_count = lax.axis_size("x")
    device_count = stn_count * sec_count
    inputs_here = voltages.shape[1]
    spectra = voltages.shape[2] // points - tap_count + 1
    filtered = polyphase(voltages, fir_taps, spectra)
    channel_of = jnp.concatenate([cor_channels, beam_channels])
    slot_gain = jnp.concatenate([cor_gain, beam_gain])
    cos_table, sin_table = lax.optimization_barrier(make_tables(channel_of, points))
    weight_re, weight_im = make_weights(beam_stations, beam_codes, STATIONS)
    spectra_all = spectrum(filtered, cos_table, sin_table, slot_gain)
    outgoing = spectra_all.reshape(2, device_count, inputs_here, 2 * spectra)
    turned = lax.all_to_all(outgoing, ALL_AXES, split_axis=1, concat_axis=1, tiled=True)
    received = turned.reshape(2, device_count * inputs_here, 2 * spectra)
    cor_data = received[0]
    beam_data = received[1:2]
    swapped = jnp.concatenate([cor_data[:, spectra:], -cor_data[:, :spectra]], axis=1)
    vis_re = contract(cor_data, cor_data) / spectra
    vis_im = contract(swapped, cor_data) / spectra
    visibilities = jnp.stack([vis_re, vis_im])[None].astype(jnp.bfloat16)
    raw_beams = form_beams(beam_data, weight_re, weight_im)
    local_power = jnp.sum(raw_beams * raw_beams, axis=(0, 2, 3))
    spread_power = jnp.broadcast_to(local_power[None], (device_count, local_power.shape[0]))
    gathered_power = lax.all_to_all(spread_power, ALL_AXES, split_axis=0, concat_axis=0, tiled=True)
    summed_power = jnp.sum(gathered_power, axis=0)
    beam_power = summed_power / (device_count * raw_beams.shape[2] * raw_beams.shape[3])
    beams = (raw_beams * lax.rsqrt(beam_power + epsilon)[None, :, None, None]).astype(jnp.bfloat16)
    return (visibilities, beams)


def solution(mesh):
    stn_count, sec_count = mesh.devices.shape
    cores = 2
    y_count = 4
    z_count = stn_count // (y_count * cores)
    devices = mesh.devices.reshape(y_count, z_count, cores, sec_count)
    fine = jax.sharding.Mesh(devices, ("y", "z", "core", "x"))
    spread = ("y", "z", "core", "x")
    in_specs = (P(None, spread, None), P(), P(), P(), P(), P(), P(), P())
    out_specs = (P(spread, None, None, None), P(spread, None, None, None))
    return jax.shard_map(
        per_device, mesh=fine, in_specs=in_specs, out_specs=out_specs, check_vma=False
    )
```

```python
import math

import jax
import jax.numpy as jnp
from jax import lax
from jax.experimental import pallas as pl
from jax.experimental.pallas import tpu as pltpu
from jax.sharding import PartitionSpec as P

STATIONS = 512


epsilon = 1e-05

STN_AXES = ("y", "z", "core")
PHYSICAL_AXES = ("core", "x", "y", "z")
ALL_AXES = ("y", "z", "core", "x")


def make_tables(channel_of, points):
    outer = 64
    inner = points // outer
    step = 2.0 * math.pi / points
    a_index = jnp.arange(inner, dtype=jnp.int32)
    b_index = jnp.arange(outer, dtype=jnp.int32)
    a_turns = (channel_of[:, None] * a_index[None, :] % inner) * outer
    b_turns = channel_of[:, None] * b_index[None, :] % points
    a_angle = a_turns.astype(jnp.float32) * step
    b_angle = b_turns.astype(jnp.float32) * step
    ca, sa = jnp.cos(a_angle)[:, :, None], jnp.sin(a_angle)[:, :, None]
    cb, sb = jnp.cos(b_angle)[:, None, :], jnp.sin(b_angle)[:, None, :]
    table_scale = 1.0 / math.sqrt(points)
    cos_table = ((ca * cb - sa * sb) * table_scale).astype(jnp.bfloat16)
    sin_table = ((sa * cb + ca * sb) * table_scale).astype(jnp.bfloat16)
    slots = channel_of.shape[0]
    return (cos_table.reshape(slots, points), sin_table.reshape(slots, points))


def make_weights(beam_stations, beam_codes, stations):
    station_ids = jnp.arange(stations, dtype=jnp.int32)
    onehot = (beam_stations[:, :, None] == station_ids[None, None, :]).astype(jnp.float32)
    amplitude = (1 + beam_codes // 64).astype(jnp.float32)
    phase_angle = (beam_codes % 64).astype(jnp.float32) * (2.0 * math.pi / 64.0)
    weight_re = jnp.einsum("bk,bks->bs", amplitude * jnp.cos(phase_angle), onehot)
    weight_im = jnp.einsum("bk,bks->bs", amplitude * jnp.sin(phase_angle), onehot)
    return (weight_re.astype(jnp.bfloat16), weight_im.astype(jnp.bfloat16))


def fir_kernel(x_ref, h_ref, o_ref, os_ref):
    tap_count = h_ref.shape[0]
    blocks, rows, lanes = x_ref.shape[1], x_ref.shape[2], x_ref.shape[3]
    inputs_here = o_ref.shape[1]
    spectra = o_ref.shape[2]
    for block in range(blocks):
        taps = [
            jnp.broadcast_to(h_ref[pl.ds(t, 1), pl.ds(block * lanes, lanes)], (rows, lanes))
            for t in range(tap_count)
        ]

        def frame_body(s, carry):
            acc = taps[0] * x_ref[s, block]
            for t in range(1, tap_count):
                acc = acc + taps[t] * x_ref[s + t, block]
            os_ref[pl.ds(s, rows, stride=spectra), :] = acc
            return carry

        lax.fori_loop(0, spectra, frame_body, 0, unroll=8)
        for r in range(rows):
            o_ref[r // inputs_here, r % inputs_here, :, pl.ds(block * lanes, lanes)] = os_ref[
                pl.ds(r * spectra, spectra), :
            ].astype(o_ref.dtype)


def polyphase(in_block, fir_taps, spectra):
    tap_count, points = fir_taps.shape
    components, inputs_here, samples = in_block.shape
    rows = components * inputs_here
    lanes = 128
    frames = samples // points
    per_frame = points // lanes
    tiles = in_block.reshape(components, inputs_here, samples // lanes, lanes)
    tiles = jnp.transpose(tiles, (2, 0, 1, 3)).astype(jnp.float32)
    tiles = tiles.reshape(frames, per_frame, rows, lanes)
    blocks = 4
    return pl.pallas_call(
        fir_kernel,
        grid=(per_frame // blocks,),
        in_specs=[
            pl.BlockSpec((frames, blocks, rows, lanes), lambda b: (0, b, 0, 0)),
            pl.BlockSpec((tap_count, blocks * lanes), lambda b: (0, b)),
        ],
        out_specs=pl.BlockSpec(
            (components, inputs_here, spectra, blocks * lanes), lambda b: (0, 0, 0, b)
        ),
        out_shape=jax.ShapeDtypeStruct((components, inputs_here, spectra, points), jnp.bfloat16),
        scratch_shapes=[pltpu.VMEM((rows * spectra, lanes), jnp.float32)],
    )(tiles, fir_taps)


def contract(left_rows, right_rows):
    contract_dims = (((1,), (1,)), ((), ()))
    return lax.dot_general(left_rows, right_rows, contract_dims, preferred_element_type=jnp.float32)


def spectrum(filtered, cos_table, sin_table, slot_gain):
    inputs_here, spectra, points = (filtered.shape[1], filtered.shape[2], filtered.shape[3])
    rows = inputs_here * spectra
    slots = cos_table.shape[0]
    tables = jnp.concatenate([cos_table, sin_table], axis=0)
    products = contract(tables, filtered.reshape(2 * rows, points))
    cos_re, cos_im = products[:slots, :rows], products[:slots, rows:]
    sin_re, sin_im = products[slots:, :rows], products[slots:, rows:]
    spec_re = cos_re + sin_im
    spec_im = cos_im - sin_re
    combined = jnp.concatenate(
        [spec_re.reshape(-1, inputs_here, spectra), spec_im.reshape(-1, inputs_here, spectra)],
        axis=2,
    )
    return (combined * slot_gain[:, None, None]).astype(jnp.bfloat16)


def form_beams(beam_data, weight_re, weight_im):
    spectra = beam_data.shape[2] // 2
    samples = beam_data.reshape(beam_data.shape[0], -1, 2, beam_data.shape[2])
    with_re = jnp.einsum("bs,jspt->jbpt", weight_re, samples, preferred_element_type=jnp.float32)
    with_im = jnp.einsum("bs,jspt->jbpt", weight_im, samples, preferred_element_type=jnp.float32)
    out_re = with_re[..., :spectra] - with_im[..., spectra:]
    out_im = with_re[..., spectra:] + with_im[..., :spectra]
    return jnp.concatenate([out_re, out_im], axis=3)


def per_device(
    voltages, fir_taps, cor_channels, beam_channels, cor_gain, beam_gain, beam_stations, beam_codes
):
    tap_count, points = fir_taps.shape
    stn_count = lax.axis_size(STN_AXES)
    sec_count = lax.axis_size("x")
    device_count = stn_count * sec_count
    inputs_here = voltages.shape[1]
    spectra = voltages.shape[2] // points - tap_count + 1
    filtered = polyphase(voltages, fir_taps, spectra)
    channel_of = jnp.concatenate([cor_channels, beam_channels])
    slot_gain = jnp.concatenate([cor_gain, beam_gain])
    cos_table, sin_table = lax.optimization_barrier(make_tables(channel_of, points))
    weight_re, weight_im = make_weights(beam_stations, beam_codes, STATIONS)
    spectra_all = spectrum(filtered, cos_table, sin_table, slot_gain)
    outgoing = spectra_all.reshape(2, device_count, inputs_here, 2 * spectra)
    turned = lax.all_to_all(outgoing, ALL_AXES, split_axis=1, concat_axis=1, tiled=True)
    received = turned.reshape(2, device_count * inputs_here, 2 * spectra)
    cor_data = received[0]
    beam_data = received[1:2]
    raw_beams = form_beams(beam_data, weight_re, weight_im)
    local_power = jnp.sum(raw_beams * raw_beams, axis=(0, 2, 3))
    spread_power = jnp.broadcast_to(local_power[None], (device_count, local_power.shape[0]))
    spread_power, cor_data = lax.optimization_barrier((spread_power, cor_data))
    gathered_power = lax.all_to_all(spread_power, ALL_AXES, split_axis=0, concat_axis=0, tiled=True)
    swapped = jnp.concatenate([cor_data[:, spectra:], -cor_data[:, :spectra]], axis=1)
    both = contract(jnp.concatenate([cor_data, swapped], axis=0), cor_data) / spectra
    visibilities = both.reshape(1, 2, cor_data.shape[0], cor_data.shape[0]).astype(jnp.bfloat16)
    summed_power = jnp.sum(gathered_power, axis=0)
    beam_power = summed_power / (device_count * raw_beams.shape[2] * raw_beams.shape[3])
    beams = (raw_beams * lax.rsqrt(beam_power + epsilon)[None, :, None, None]).astype(jnp.bfloat16)
    return (visibilities, beams)


def solution(mesh):
    stn_count, sec_count = mesh.devices.shape
    cores = 2
    y_count = 4
    z_count = stn_count // (y_count * cores)
    devices = mesh.devices.reshape(y_count, z_count, cores, sec_count)
    fine = jax.sharding.Mesh(devices, ("y", "z", "core", "x"))
    spread = ("y", "z", "core", "x")
    in_specs = (P(None, spread, None), P(), P(), P(), P(), P(), P(), P())
    out_specs = (P(spread, None, None, None), P(spread, None, None, None))
    return jax.shard_map(
        per_device, mesh=fine, in_specs=in_specs, out_specs=out_specs, check_vma=False
    )
```

```python
import math

import jax
import jax.numpy as jnp
from jax import lax
from jax.experimental import pallas as pl
from jax.experimental.pallas import tpu as pltpu
from jax.sharding import PartitionSpec as P

STATIONS = 512


epsilon = 1e-05

STN_AXES = ("y", "z", "core")
PHYSICAL_AXES = ("core", "x", "y", "z")
ALL_AXES = ("y", "z", "core", "x")


def make_tables(channel_of, points):
    outer = 64
    inner = points // outer
    step = 2.0 * math.pi / points
    a_index = jnp.arange(inner, dtype=jnp.int32)
    b_index = jnp.arange(outer, dtype=jnp.int32)
    a_turns = (channel_of[:, None] * a_index[None, :] % inner) * outer
    b_turns = channel_of[:, None] * b_index[None, :] % points
    a_angle = a_turns.astype(jnp.float32) * step
    b_angle = b_turns.astype(jnp.float32) * step
    ca, sa = jnp.cos(a_angle)[:, :, None], jnp.sin(a_angle)[:, :, None]
    cb, sb = jnp.cos(b_angle)[:, None, :], jnp.sin(b_angle)[:, None, :]
    table_scale = 1.0 / math.sqrt(points)
    cos_table = ((ca * cb - sa * sb) * table_scale).astype(jnp.bfloat16)
    sin_table = ((sa * cb + ca * sb) * table_scale).astype(jnp.bfloat16)
    slots = channel_of.shape[0]
    return (cos_table.reshape(slots, points), sin_table.reshape(slots, points))


def make_weights(beam_stations, beam_codes, stations):
    station_ids = jnp.arange(stations, dtype=jnp.int32)
    onehot = (beam_stations[:, :, None] == station_ids[None, None, :]).astype(jnp.float32)
    amplitude = (1 + beam_codes // 64).astype(jnp.float32)
    phase_angle = (beam_codes % 64).astype(jnp.float32) * (2.0 * math.pi / 64.0)
    weight_re = jnp.einsum("bk,bks->bs", amplitude * jnp.cos(phase_angle), onehot)
    weight_im = jnp.einsum("bk,bks->bs", amplitude * jnp.sin(phase_angle), onehot)
    return (weight_re.astype(jnp.bfloat16), weight_im.astype(jnp.bfloat16))


def fir_kernel(x_ref, h_ref, o_ref, os_ref):
    tap_count = h_ref.shape[0]
    blocks, rows, lanes = x_ref.shape[1], x_ref.shape[2], x_ref.shape[3]
    inputs_here = o_ref.shape[1]
    spectra = o_ref.shape[2]
    for block in range(blocks):
        taps = [
            jnp.broadcast_to(h_ref[pl.ds(t, 1), pl.ds(block * lanes, lanes)], (rows, lanes))
            for t in range(tap_count)
        ]

        def frame_body(s, carry):
            acc = taps[0] * x_ref[s, block]
            for t in range(1, tap_count):
                acc = acc + taps[t] * x_ref[s + t, block]
            os_ref[pl.ds(s, rows, stride=spectra), :] = acc
            return carry

        lax.fori_loop(0, spectra, frame_body, 0, unroll=8)
        for r in range(rows):
            o_ref[r // inputs_here, r % inputs_here, :, pl.ds(block * lanes, lanes)] = os_ref[
                pl.ds(r * spectra, spectra), :
            ].astype(o_ref.dtype)


def polyphase(in_block, fir_taps, spectra):
    tap_count, points = fir_taps.shape
    components, inputs_here, samples = in_block.shape
    rows = components * inputs_here
    lanes = 128
    frames = samples // points
    per_frame = points // lanes
    tiles = in_block.reshape(components, inputs_here, samples // lanes, lanes)
    tiles = jnp.transpose(tiles, (2, 0, 1, 3)).astype(jnp.float32)
    tiles = tiles.reshape(frames, per_frame, rows, lanes)
    blocks = 4
    return pl.pallas_call(
        fir_kernel,
        grid=(per_frame // blocks,),
        in_specs=[
            pl.BlockSpec((frames, blocks, rows, lanes), lambda b: (0, b, 0, 0)),
            pl.BlockSpec((tap_count, blocks * lanes), lambda b: (0, b)),
        ],
        out_specs=pl.BlockSpec(
            (components, inputs_here, spectra, blocks * lanes), lambda b: (0, 0, 0, b)
        ),
        out_shape=jax.ShapeDtypeStruct((components, inputs_here, spectra, points), jnp.bfloat16),
        scratch_shapes=[pltpu.VMEM((rows * spectra, lanes), jnp.float32)],
    )(tiles, fir_taps)


def contract(left_rows, right_rows):
    contract_dims = (((1,), (1,)), ((), ()))
    return lax.dot_general(left_rows, right_rows, contract_dims, preferred_element_type=jnp.float32)


def spectrum(filtered, cos_table, sin_table, slot_gain):
    inputs_here, spectra, points = (filtered.shape[1], filtered.shape[2], filtered.shape[3])
    rows = inputs_here * spectra
    slots = cos_table.shape[0]
    tables = jnp.concatenate([cos_table, sin_table], axis=0)
    products = contract(tables, filtered.reshape(2 * rows, points))
    cos_re, cos_im = products[:slots, :rows], products[:slots, rows:]
    sin_re, sin_im = products[slots:, :rows], products[slots:, rows:]
    spec_re = cos_re + sin_im
    spec_im = cos_im - sin_re
    combined = jnp.concatenate(
        [spec_re.reshape(-1, inputs_here, spectra), spec_im.reshape(-1, inputs_here, spectra)],
        axis=2,
    )
    return (combined * slot_gain[:, None, None]).astype(jnp.bfloat16)


def form_beams(beam_data, weight_re, weight_im):
    spectra = beam_data.shape[2] // 2
    samples = beam_data.reshape(beam_data.shape[0], -1, 2, beam_data.shape[2])
    with_re = jnp.einsum("bs,jspt->jbpt", weight_re, samples, preferred_element_type=jnp.float32)
    with_im = jnp.einsum("bs,jspt->jbpt", weight_im, samples, preferred_element_type=jnp.float32)
    out_re = with_re[..., :spectra] - with_im[..., spectra:]
    out_im = with_re[..., spectra:] + with_im[..., :spectra]
    return jnp.concatenate([out_re, out_im], axis=3)


def per_device(
    voltages, fir_taps, cor_channels, beam_channels, cor_gain, beam_gain, beam_stations, beam_codes
):
    tap_count, points = fir_taps.shape
    stn_count = lax.axis_size(STN_AXES)
    sec_count = lax.axis_size("x")
    device_count = stn_count * sec_count
    inputs_here = voltages.shape[1]
    spectra = voltages.shape[2] // points - tap_count + 1
    filtered = polyphase(voltages, fir_taps, spectra)
    channel_of = jnp.stack([cor_channels, beam_channels], axis=1).reshape(-1)
    slot_gain = jnp.stack([cor_gain, beam_gain], axis=1).reshape(-1)
    cos_table, sin_table = lax.optimization_barrier(make_tables(channel_of, points))
    weight_re, weight_im = make_weights(beam_stations, beam_codes, STATIONS)
    spectra_all = spectrum(filtered, cos_table, sin_table, slot_gain)
    outgoing = spectra_all.reshape(device_count, 2, inputs_here, 2 * spectra)
    turned = lax.all_to_all(outgoing, ALL_AXES, split_axis=0, concat_axis=0, tiled=True)
    cor_data = turned[:, 0].reshape(device_count * inputs_here, 2 * spectra)
    beam_data = turned[:, 1].reshape(1, device_count * inputs_here, 2 * spectra)
    raw_beams = form_beams(beam_data, weight_re, weight_im)
    local_power = jnp.sum(raw_beams * raw_beams, axis=(0, 2, 3))
    spread_power = jnp.broadcast_to(local_power[None], (device_count, local_power.shape[0]))
    spread_power, cor_data = lax.optimization_barrier((spread_power, cor_data))
    gathered_power = lax.all_to_all(spread_power, ALL_AXES, split_axis=0, concat_axis=0, tiled=True)
    swapped = jnp.concatenate([cor_data[:, spectra:], -cor_data[:, :spectra]], axis=1)
    both = contract(jnp.concatenate([cor_data, swapped], axis=0), cor_data) / spectra
    visibilities = both.reshape(1, 2, cor_data.shape[0], cor_data.shape[0]).astype(jnp.bfloat16)
    summed_power = jnp.sum(gathered_power, axis=0)
    beam_power = summed_power / (device_count * raw_beams.shape[2] * raw_beams.shape[3])
    beams = (raw_beams * lax.rsqrt(beam_power + epsilon)[None, :, None, None]).astype(jnp.bfloat16)
    return (visibilities, beams)


def solution(mesh):
    stn_count, sec_count = mesh.devices.shape
    cores = 2
    y_count = 4
    z_count = stn_count // (y_count * cores)
    devices = mesh.devices.reshape(y_count, z_count, cores, sec_count)
    fine = jax.sharding.Mesh(devices, ("y", "z", "core", "x"))
    spread = ("y", "z", "core", "x")
    in_specs = (P(None, spread, None), P(), P(), P(), P(), P(), P(), P())
    out_specs = (P(spread, None, None, None), P(spread, None, None, None))
    return jax.shard_map(
        per_device, mesh=fine, in_specs=in_specs, out_specs=out_specs, check_vma=False
    )
```

```python
import math

import jax
import jax.numpy as jnp
from jax import lax
from jax.experimental import pallas as pl
from jax.experimental.pallas import tpu as pltpu
from jax.sharding import PartitionSpec as P

STATIONS = 512


epsilon = 1e-05

STN_AXES = ("y", "z", "core")
PHYSICAL_AXES = ("core", "x", "y", "z")
ALL_AXES = ("y", "z", "core", "x")


def make_tables(channel_of, points):
    outer = 64
    inner = points // outer
    step = 2.0 * math.pi / points
    a_index = jnp.arange(inner, dtype=jnp.int32)
    b_index = jnp.arange(outer, dtype=jnp.int32)
    a_turns = (channel_of[:, None] * a_index[None, :] % inner) * outer
    b_turns = channel_of[:, None] * b_index[None, :] % points
    a_angle = a_turns.astype(jnp.float32) * step
    b_angle = b_turns.astype(jnp.float32) * step
    table_scale = 1.0 / math.sqrt(points)
    ca = (jnp.cos(a_angle) * table_scale)[:, :, None]
    sa = (jnp.sin(a_angle) * table_scale)[:, :, None]
    cb, sb = jnp.cos(b_angle)[:, None, :], jnp.sin(b_angle)[:, None, :]
    cos_table = (ca * cb - sa * sb).astype(jnp.bfloat16)
    sin_table = (sa * cb + ca * sb).astype(jnp.bfloat16)
    slots = channel_of.shape[0]
    return (cos_table.reshape(slots, points), sin_table.reshape(slots, points))


def make_weights(beam_stations, beam_codes, stations):
    station_ids = jnp.arange(stations, dtype=jnp.int32)
    onehot = (beam_stations[:, :, None] == station_ids[None, None, :]).astype(jnp.float32)
    amplitude = (1 + beam_codes // 64).astype(jnp.float32)
    phase_angle = (beam_codes % 64).astype(jnp.float32) * (2.0 * math.pi / 64.0)
    weight_re = jnp.einsum("bk,bks->bs", amplitude * jnp.cos(phase_angle), onehot)
    weight_im = jnp.einsum("bk,bks->bs", amplitude * jnp.sin(phase_angle), onehot)
    return (weight_re.astype(jnp.bfloat16), weight_im.astype(jnp.bfloat16))


def fir_kernel(x_ref, h_ref, o_ref, os_ref):
    tap_count = h_ref.shape[0]
    blocks, rows, lanes = x_ref.shape[1], x_ref.shape[2], x_ref.shape[3]
    inputs_here = o_ref.shape[1]
    spectra = o_ref.shape[2]
    for block in range(blocks):
        taps = [
            jnp.broadcast_to(h_ref[pl.ds(t, 1), pl.ds(block * lanes, lanes)], (rows, lanes))
            for t in range(tap_count)
        ]

        def frame_body(s, carry):
            acc = taps[0] * x_ref[s, block]
            for t in range(1, tap_count):
                acc = acc + taps[t] * x_ref[s + t, block]
            os_ref[pl.ds(s, rows, stride=spectra), :] = acc
            return carry

        lax.fori_loop(0, spectra, frame_body, 0, unroll=8)
        for r in range(rows):
            o_ref[r // inputs_here, r % inputs_here, :, pl.ds(block * lanes, lanes)] = os_ref[
                pl.ds(r * spectra, spectra), :
            ].astype(o_ref.dtype)


def polyphase(in_block, fir_taps, spectra):
    tap_count, points = fir_taps.shape
    components, inputs_here, samples = in_block.shape
    rows = components * inputs_here
    lanes = 128
    frames = samples // points
    per_frame = points // lanes
    tiles = in_block.reshape(components, inputs_here, samples // lanes, lanes)
    tiles = jnp.transpose(tiles, (2, 0, 1, 3)).astype(jnp.float32)
    tiles = tiles.reshape(frames, per_frame, rows, lanes)
    blocks = 4
    return pl.pallas_call(
        fir_kernel,
        grid=(per_frame // blocks,),
        in_specs=[
            pl.BlockSpec((frames, blocks, rows, lanes), lambda b: (0, b, 0, 0)),
            pl.BlockSpec((tap_count, blocks * lanes), lambda b: (0, b)),
        ],
        out_specs=pl.BlockSpec(
            (components, inputs_here, spectra, blocks * lanes), lambda b: (0, 0, 0, b)
        ),
        out_shape=jax.ShapeDtypeStruct((components, inputs_here, spectra, points), jnp.bfloat16),
        scratch_shapes=[pltpu.VMEM((rows * spectra, lanes), jnp.float32)],
    )(tiles, fir_taps)


def contract(left_rows, right_rows):
    contract_dims = (((1,), (1,)), ((), ()))
    return lax.dot_general(left_rows, right_rows, contract_dims, preferred_element_type=jnp.float32)


def spectrum(filtered, cos_table, sin_table, slot_gain):
    inputs_here, spectra, points = (filtered.shape[1], filtered.shape[2], filtered.shape[3])
    rows = inputs_here * spectra
    slots = cos_table.shape[0]
    tables = jnp.concatenate([cos_table, sin_table], axis=0)
    products = contract(tables, filtered.reshape(2 * rows, points))
    cos_re, cos_im = products[:slots, :rows], products[:slots, rows:]
    sin_re, sin_im = products[slots:, :rows], products[slots:, rows:]
    spec_re = cos_re + sin_im
    spec_im = cos_im - sin_re
    combined = jnp.concatenate(
        [spec_re.reshape(-1, inputs_here, spectra), spec_im.reshape(-1, inputs_here, spectra)],
        axis=2,
    )
    return (combined * slot_gain[:, None, None]).astype(jnp.bfloat16)


def form_beams(beam_data, weight_re, weight_im):
    spectra = beam_data.shape[2] // 2
    samples = beam_data.reshape(beam_data.shape[0], -1, 2, beam_data.shape[2])
    with_re = jnp.einsum("bs,jspt->jbpt", weight_re, samples, preferred_element_type=jnp.float32)
    with_im = jnp.einsum("bs,jspt->jbpt", weight_im, samples, preferred_element_type=jnp.float32)
    out_re = with_re[..., :spectra] - with_im[..., spectra:]
    out_im = with_re[..., spectra:] + with_im[..., :spectra]
    return jnp.concatenate([out_re, out_im], axis=3)


def per_device(
    voltages, fir_taps, cor_channels, beam_channels, cor_gain, beam_gain, beam_stations, beam_codes
):
    tap_count, points = fir_taps.shape
    stn_count = lax.axis_size(STN_AXES)
    sec_count = lax.axis_size("x")
    device_count = stn_count * sec_count
    inputs_here = voltages.shape[1]
    spectra = voltages.shape[2] // points - tap_count + 1
    filtered = polyphase(voltages, fir_taps, spectra)
    channel_of = jnp.stack([cor_channels, beam_channels], axis=1).reshape(-1)
    slot_gain = jnp.stack([cor_gain, beam_gain], axis=1).reshape(-1)
    cos_table, sin_table = lax.optimization_barrier(make_tables(channel_of, points))
    weight_re, weight_im = make_weights(beam_stations, beam_codes, STATIONS)
    spectra_all = spectrum(filtered, cos_table, sin_table, slot_gain)
    outgoing = spectra_all.reshape(device_count, 2, inputs_here, 2 * spectra)
    turned = lax.all_to_all(outgoing, ALL_AXES, split_axis=0, concat_axis=0, tiled=True)
    cor_data = turned[:, 0].reshape(device_count * inputs_here, 2 * spectra)
    beam_data = turned[:, 1].reshape(1, device_count * inputs_here, 2 * spectra)
    raw_beams = form_beams(beam_data, weight_re, weight_im)
    local_power = jnp.sum(raw_beams * raw_beams, axis=(0, 2, 3))
    spread_power = jnp.broadcast_to(local_power[None], (device_count, local_power.shape[0]))
    spread_power, cor_data = lax.optimization_barrier((spread_power, cor_data))
    gathered_power = lax.all_to_all(spread_power, ALL_AXES, split_axis=0, concat_axis=0, tiled=True)
    swapped = jnp.concatenate([cor_data[:, spectra:], -cor_data[:, :spectra]], axis=1)
    both = contract(jnp.concatenate([cor_data, swapped], axis=0), cor_data) / spectra
    visibilities = both.reshape(1, 2, cor_data.shape[0], cor_data.shape[0]).astype(jnp.bfloat16)
    summed_power = jnp.sum(gathered_power, axis=0)
    beam_power = summed_power / (device_count * raw_beams.shape[2] * raw_beams.shape[3])
    beams = (raw_beams * lax.rsqrt(beam_power + epsilon)[None, :, None, None]).astype(jnp.bfloat16)
    return (visibilities, beams)


def solution(mesh):
    stn_count, sec_count = mesh.devices.shape
    cores = 2
    y_count = 4
    z_count = stn_count // (y_count * cores)
    devices = mesh.devices.reshape(y_count, z_count, cores, sec_count)
    fine = jax.sharding.Mesh(devices, ("y", "z", "core", "x"))
    spread = ("y", "z", "core", "x")
    in_specs = (P(None, spread, None), P(), P(), P(), P(), P(), P(), P())
    out_specs = (P(spread, None, None, None), P(spread, None, None, None))
    return jax.shard_map(
        per_device, mesh=fine, in_specs=in_specs, out_specs=out_specs, check_vma=False
    )
```

```python
import math

import jax
import jax.numpy as jnp
from jax import lax
from jax.experimental import pallas as pl
from jax.experimental.pallas import tpu as pltpu
from jax.sharding import PartitionSpec as P

STATIONS = 512


epsilon = 1e-05

STN_AXES = ("y", "z", "core")
PHYSICAL_AXES = ("core", "x", "y", "z")
ALL_AXES = ("y", "z", "core", "x")


def make_tables(channel_of, points):
    outer = 64
    inner = points // outer
    step = 2.0 * math.pi / points
    a_index = jnp.arange(inner, dtype=jnp.int32)
    b_index = jnp.arange(outer, dtype=jnp.int32)
    a_turns = (channel_of[:, None] * a_index[None, :] % inner) * outer
    b_turns = channel_of[:, None] * b_index[None, :] % points
    a_angle = a_turns.astype(jnp.float32) * step
    b_angle = b_turns.astype(jnp.float32) * step
    ca, sa = jnp.cos(a_angle)[:, :, None], jnp.sin(a_angle)[:, :, None]
    cb, sb = jnp.cos(b_angle)[:, None, :], jnp.sin(b_angle)[:, None, :]
    table_scale = 1.0 / math.sqrt(points)
    cos_table = ((ca * cb - sa * sb) * table_scale).astype(jnp.bfloat16)
    sin_table = ((sa * cb + ca * sb) * table_scale).astype(jnp.bfloat16)
    slots = channel_of.shape[0]
    return (cos_table.reshape(slots, points), sin_table.reshape(slots, points))


def make_weights(beam_stations, beam_codes, stations):
    station_ids = jnp.arange(stations, dtype=jnp.int32)
    onehot = (beam_stations[:, :, None] == station_ids[None, None, :]).astype(jnp.float32)
    amplitude = (1 + beam_codes // 64).astype(jnp.float32)
    phase_angle = (beam_codes % 64).astype(jnp.float32) * (2.0 * math.pi / 64.0)
    weight_re = jnp.einsum("bk,bks->bs", amplitude * jnp.cos(phase_angle), onehot)
    weight_im = jnp.einsum("bk,bks->bs", amplitude * jnp.sin(phase_angle), onehot)
    return (weight_re.astype(jnp.bfloat16), weight_im.astype(jnp.bfloat16))


def fir_kernel(x_ref, h_ref, o_ref, os_ref):
    tap_count = h_ref.shape[0]
    blocks, rows, lanes = x_ref.shape[1], x_ref.shape[2], x_ref.shape[3]
    inputs_here = o_ref.shape[1]
    spectra = o_ref.shape[2]
    for block in range(blocks):
        taps = [
            jnp.broadcast_to(h_ref[pl.ds(t, 1), pl.ds(block * lanes, lanes)], (rows, lanes))
            for t in range(tap_count)
        ]

        def frame_body(step, carry):
            first = pl.multiple_of(step * 8, 8)
            window = [
                x_ref[first + f, block].astype(jnp.float32) for f in range(8 + tap_count - 1)
            ]
            for k in range(8):
                acc = taps[0] * window[k]
                for t in range(1, tap_count):
                    acc = acc + taps[t] * window[k + t]
                os_ref[pl.ds(first + k, rows, stride=spectra), :] = acc
            return carry

        lax.fori_loop(0, spectra // 8, frame_body, 0)
        for r in range(rows):
            o_ref[r // inputs_here, r % inputs_here, :, pl.ds(block * lanes, lanes)] = os_ref[
                pl.ds(r * spectra, spectra), :
            ].astype(o_ref.dtype)


def polyphase(in_block, fir_taps, spectra):
    tap_count, points = fir_taps.shape
    components, inputs_here, samples = in_block.shape
    rows = components * inputs_here
    lanes = 128
    frames = samples // points
    per_frame = points // lanes
    tiles = in_block.reshape(components, inputs_here, samples // lanes, lanes)
    tiles = jnp.transpose(tiles, (2, 0, 1, 3))
    tiles = tiles.reshape(frames, per_frame, rows, lanes)
    blocks = 4
    return pl.pallas_call(
        fir_kernel,
        grid=(per_frame // blocks,),
        in_specs=[
            pl.BlockSpec((frames, blocks, rows, lanes), lambda b: (0, b, 0, 0)),
            pl.BlockSpec((tap_count, blocks * lanes), lambda b: (0, b)),
        ],
        out_specs=pl.BlockSpec(
            (components, inputs_here, spectra, blocks * lanes), lambda b: (0, 0, 0, b)
        ),
        out_shape=jax.ShapeDtypeStruct((components, inputs_here, spectra, points), jnp.bfloat16),
        scratch_shapes=[pltpu.VMEM((rows * spectra, lanes), jnp.float32)],
    )(tiles, fir_taps)


def contract(left_rows, right_rows):
    contract_dims = (((1,), (1,)), ((), ()))
    return lax.dot_general(left_rows, right_rows, contract_dims, preferred_element_type=jnp.float32)


def spectrum(filtered, cos_table, sin_table, slot_gain):
    inputs_here, spectra, points = (filtered.shape[1], filtered.shape[2], filtered.shape[3])
    rows = inputs_here * spectra
    slots = cos_table.shape[0]
    tables = jnp.concatenate([cos_table, sin_table], axis=0)
    products = contract(tables, filtered.reshape(2 * rows, points))
    cos_re, cos_im = products[:slots, :rows], products[:slots, rows:]
    sin_re, sin_im = products[slots:, :rows], products[slots:, rows:]
    spec_re = cos_re + sin_im
    spec_im = cos_im - sin_re
    combined = jnp.concatenate(
        [spec_re.reshape(-1, inputs_here, spectra), spec_im.reshape(-1, inputs_here, spectra)],
        axis=2,
    )
    return (combined * slot_gain[:, None, None]).astype(jnp.bfloat16)


def form_beams(beam_data, weight_re, weight_im):
    spectra = beam_data.shape[2] // 2
    samples = beam_data.reshape(beam_data.shape[0], -1, 2, beam_data.shape[2])
    with_re = jnp.einsum("bs,jspt->jbpt", weight_re, samples, preferred_element_type=jnp.float32)
    with_im = jnp.einsum("bs,jspt->jbpt", weight_im, samples, preferred_element_type=jnp.float32)
    out_re = with_re[..., :spectra] - with_im[..., spectra:]
    out_im = with_re[..., spectra:] + with_im[..., :spectra]
    return jnp.concatenate([out_re, out_im], axis=3)


def per_device(
    voltages, fir_taps, cor_channels, beam_channels, cor_gain, beam_gain, beam_stations, beam_codes
):
    tap_count, points = fir_taps.shape
    stn_count = lax.axis_size(STN_AXES)
    sec_count = lax.axis_size("x")
    device_count = stn_count * sec_count
    inputs_here = voltages.shape[1]
    spectra = voltages.shape[2] // points - tap_count + 1
    filtered = polyphase(voltages, fir_taps, spectra)
    channel_of = jnp.stack([cor_channels, beam_channels], axis=1).reshape(-1)
    slot_gain = jnp.stack([cor_gain, beam_gain], axis=1).reshape(-1)
    cos_table, sin_table = lax.optimization_barrier(make_tables(channel_of, points))
    weight_re, weight_im = make_weights(beam_stations, beam_codes, STATIONS)
    spectra_all = spectrum(filtered, cos_table, sin_table, slot_gain)
    outgoing = spectra_all.reshape(device_count, 2, inputs_here, 2 * spectra)
    turned = lax.all_to_all(outgoing, ALL_AXES, split_axis=0, concat_axis=0, tiled=True)
    cor_data = turned[:, 0].reshape(device_count * inputs_here, 2 * spectra)
    beam_data = turned[:, 1].reshape(1, device_count * inputs_here, 2 * spectra)
    raw_beams = form_beams(beam_data, weight_re, weight_im)
    local_power = jnp.sum(raw_beams * raw_beams, axis=(0, 2, 3))
    spread_power = jnp.broadcast_to(local_power[None], (device_count, local_power.shape[0]))
    spread_power, cor_data = lax.optimization_barrier((spread_power, cor_data))
    gathered_power = lax.all_to_all(spread_power, ALL_AXES, split_axis=0, concat_axis=0, tiled=True)
    swapped = jnp.concatenate([cor_data[:, spectra:], -cor_data[:, :spectra]], axis=1)
    both = contract(jnp.concatenate([cor_data, swapped], axis=0), cor_data) / spectra
    visibilities = both.reshape(1, 2, cor_data.shape[0], cor_data.shape[0]).astype(jnp.bfloat16)
    summed_power = jnp.sum(gathered_power, axis=0)
    beam_power = summed_power / (device_count * raw_beams.shape[2] * raw_beams.shape[3])
    beams = (raw_beams * lax.rsqrt(beam_power + epsilon)[None, :, None, None]).astype(jnp.bfloat16)
    return (visibilities, beams)


def solution(mesh):
    stn_count, sec_count = mesh.devices.shape
    cores = 2
    y_count = 4
    z_count = stn_count // (y_count * cores)
    devices = mesh.devices.reshape(y_count, z_count, cores, sec_count)
    fine = jax.sharding.Mesh(devices, ("y", "z", "core", "x"))
    spread = ("y", "z", "core", "x")
    in_specs = (P(None, spread, None), P(), P(), P(), P(), P(), P(), P())
    out_specs = (P(spread, None, None, None), P(spread, None, None, None))
    return jax.shard_map(
        per_device, mesh=fine, in_specs=in_specs, out_specs=out_specs, check_vma=False
    )
```

```python
import math

import jax
import jax.numpy as jnp
from jax import lax
from jax.experimental import pallas as pl
from jax.experimental.pallas import tpu as pltpu
from jax.sharding import PartitionSpec as P

STATIONS = 512


epsilon = 1e-05

STN_AXES = ("y", "z", "core")
PHYSICAL_AXES = ("core", "x", "y", "z")
ALL_AXES = ("y", "z", "core", "x")


def make_tables(channel_of, points):
    outer = 64
    inner = points // outer
    step = 2.0 * math.pi / points
    a_index = jnp.arange(inner, dtype=jnp.int32)
    b_index = jnp.arange(outer, dtype=jnp.int32)
    a_turns = (channel_of[:, None] * a_index[None, :] % inner) * outer
    b_turns = channel_of[:, None] * b_index[None, :] % points
    a_angle = a_turns.astype(jnp.float32) * step
    b_angle = b_turns.astype(jnp.float32) * step
    ca, sa = jnp.cos(a_angle)[:, :, None], jnp.sin(a_angle)[:, :, None]
    cb, sb = jnp.cos(b_angle)[:, None, :], jnp.sin(b_angle)[:, None, :]
    table_scale = 1.0 / math.sqrt(points)
    cos_table = ((ca * cb - sa * sb) * table_scale).astype(jnp.bfloat16)
    sin_table = ((sa * cb + ca * sb) * table_scale).astype(jnp.bfloat16)
    slots = channel_of.shape[0]
    return (cos_table.reshape(slots, points), sin_table.reshape(slots, points))


def make_weights(beam_stations, beam_codes, stations):
    station_ids = jnp.arange(stations, dtype=jnp.int32)
    onehot = (beam_stations[:, :, None] == station_ids[None, None, :]).astype(jnp.float32)
    amplitude = (1 + beam_codes // 64).astype(jnp.float32)
    phase_angle = (beam_codes % 64).astype(jnp.float32) * (2.0 * math.pi / 64.0)
    weight_re = jnp.einsum("bk,bks->bs", amplitude * jnp.cos(phase_angle), onehot)
    weight_im = jnp.einsum("bk,bks->bs", amplitude * jnp.sin(phase_angle), onehot)
    return (weight_re.astype(jnp.bfloat16), weight_im.astype(jnp.bfloat16))


def fir_kernel(x_ref, h_ref, o_ref, os_ref):
    tap_count = h_ref.shape[0]
    blocks, rows, lanes = x_ref.shape[1], x_ref.shape[2], x_ref.shape[3]
    inputs_here = o_ref.shape[1]
    spectra = o_ref.shape[2]
    for block in range(blocks):
        taps = [
            jnp.broadcast_to(h_ref[pl.ds(t, 1), pl.ds(block * lanes, lanes)], (rows, lanes))
            for t in range(tap_count)
        ]

        def frame_body(step, carry):
            first = pl.multiple_of(step * 8, 8)
            window = [
                x_ref[first + f, block].astype(jnp.float32) for f in range(8 + tap_count - 1)
            ]
            for k in range(8):
                acc = taps[0] * window[k]
                for t in range(1, tap_count):
                    acc = acc + taps[t] * window[k + t]
                os_ref[pl.ds(first + k, rows, stride=spectra), :] = acc
            return carry

        lax.fori_loop(0, spectra // 8, frame_body, 0)
        for r in range(rows):
            o_ref[r // inputs_here, r % inputs_here, :, pl.ds(block * lanes, lanes)] = os_ref[
                pl.ds(r * spectra, spectra), :
            ].astype(o_ref.dtype)


def polyphase(in_block, fir_taps, spectra):
    tap_count, points = fir_taps.shape
    components, inputs_here, samples = in_block.shape
    rows = components * inputs_here
    lanes = 128
    frames = samples // points
    per_frame = points // lanes
    tiles = in_block.reshape(components, inputs_here, samples // lanes, lanes)
    tiles = jnp.transpose(tiles, (2, 0, 1, 3))
    tiles = tiles.reshape(frames, per_frame, rows, lanes)
    blocks = 8
    return pl.pallas_call(
        fir_kernel,
        grid=(per_frame // blocks,),
        in_specs=[
            pl.BlockSpec((frames, blocks, rows, lanes), lambda b: (0, b, 0, 0)),
            pl.BlockSpec((tap_count, blocks * lanes), lambda b: (0, b)),
        ],
        out_specs=pl.BlockSpec(
            (components, inputs_here, spectra, blocks * lanes), lambda b: (0, 0, 0, b)
        ),
        out_shape=jax.ShapeDtypeStruct((components, inputs_here, spectra, points), jnp.bfloat16),
        scratch_shapes=[pltpu.VMEM((rows * spectra, lanes), jnp.float32)],
    )(tiles, fir_taps)


def contract(left_rows, right_rows):
    contract_dims = (((1,), (1,)), ((), ()))
    return lax.dot_general(left_rows, right_rows, contract_dims, preferred_element_type=jnp.float32)


def spectrum(filtered, cos_table, sin_table, slot_gain):
    inputs_here, spectra, points = (filtered.shape[1], filtered.shape[2], filtered.shape[3])
    rows = inputs_here * spectra
    slots = cos_table.shape[0]
    tables = jnp.concatenate([cos_table, sin_table], axis=0)
    products = contract(tables, filtered.reshape(2 * rows, points))
    cos_re, cos_im = products[:slots, :rows], products[:slots, rows:]
    sin_re, sin_im = products[slots:, :rows], products[slots:, rows:]
    spec_re = cos_re + sin_im
    spec_im = cos_im - sin_re
    combined = jnp.concatenate(
        [spec_re.reshape(-1, inputs_here, spectra), spec_im.reshape(-1, inputs_here, spectra)],
        axis=2,
    )
    return (combined * slot_gain[:, None, None]).astype(jnp.bfloat16)


def form_beams(beam_data, weight_re, weight_im):
    spectra = beam_data.shape[2] // 2
    samples = beam_data.reshape(beam_data.shape[0], -1, 2, beam_data.shape[2])
    with_re = jnp.einsum("bs,jspt->jbpt", weight_re, samples, preferred_element_type=jnp.float32)
    with_im = jnp.einsum("bs,jspt->jbpt", weight_im, samples, preferred_element_type=jnp.float32)
    out_re = with_re[..., :spectra] - with_im[..., spectra:]
    out_im = with_re[..., spectra:] + with_im[..., :spectra]
    return jnp.concatenate([out_re, out_im], axis=3)


def per_device(
    voltages, fir_taps, cor_channels, beam_channels, cor_gain, beam_gain, beam_stations, beam_codes
):
    tap_count, points = fir_taps.shape
    stn_count = lax.axis_size(STN_AXES)
    sec_count = lax.axis_size("x")
    device_count = stn_count * sec_count
    inputs_here = voltages.shape[1]
    spectra = voltages.shape[2] // points - tap_count + 1
    filtered = polyphase(voltages, fir_taps, spectra)
    channel_of = jnp.stack([cor_channels, beam_channels], axis=1).reshape(-1)
    slot_gain = jnp.stack([cor_gain, beam_gain], axis=1).reshape(-1)
    cos_table, sin_table = lax.optimization_barrier(make_tables(channel_of, points))
    weight_re, weight_im = make_weights(beam_stations, beam_codes, STATIONS)
    spectra_all = spectrum(filtered, cos_table, sin_table, slot_gain)
    outgoing = spectra_all.reshape(device_count, 2, inputs_here, 2 * spectra)
    turned = lax.all_to_all(outgoing, ALL_AXES, split_axis=0, concat_axis=0, tiled=True)
    cor_data = turned[:, 0].reshape(device_count * inputs_here, 2 * spectra)
    beam_data = turned[:, 1].reshape(1, device_count * inputs_here, 2 * spectra)
    raw_beams = form_beams(beam_data, weight_re, weight_im)
    local_power = jnp.sum(raw_beams * raw_beams, axis=(0, 2, 3))
    spread_power = jnp.broadcast_to(local_power[None], (device_count, local_power.shape[0]))
    spread_power, cor_data = lax.optimization_barrier((spread_power, cor_data))
    gathered_power = lax.all_to_all(spread_power, ALL_AXES, split_axis=0, concat_axis=0, tiled=True)
    swapped = jnp.concatenate([cor_data[:, spectra:], -cor_data[:, :spectra]], axis=1)
    both = contract(jnp.concatenate([cor_data, swapped], axis=0), cor_data) / spectra
    visibilities = both.reshape(1, 2, cor_data.shape[0], cor_data.shape[0]).astype(jnp.bfloat16)
    summed_power = jnp.sum(gathered_power, axis=0)
    beam_power = summed_power / (device_count * raw_beams.shape[2] * raw_beams.shape[3])
    beams = (raw_beams * lax.rsqrt(beam_power + epsilon)[None, :, None, None]).astype(jnp.bfloat16)
    return (visibilities, beams)


def solution(mesh):
    stn_count, sec_count = mesh.devices.shape
    cores = 2
    y_count = 4
    z_count = stn_count // (y_count * cores)
    devices = mesh.devices.reshape(y_count, z_count, cores, sec_count)
    fine = jax.sharding.Mesh(devices, ("y", "z", "core", "x"))
    spread = ("y", "z", "core", "x")
    in_specs = (P(None, spread, None), P(), P(), P(), P(), P(), P(), P())
    out_specs = (P(spread, None, None, None), P(spread, None, None, None))
    return jax.shard_map(
        per_device, mesh=fine, in_specs=in_specs, out_specs=out_specs, check_vma=False
    )
```

```python
import math

import jax
import jax.numpy as jnp
from jax import lax
from jax.experimental import pallas as pl
from jax.experimental.pallas import tpu as pltpu
from jax.sharding import PartitionSpec as P

STATIONS = 512


epsilon = 1e-05

STN_AXES = ("y", "z", "core")
PHYSICAL_AXES = ("core", "x", "y", "z")
ALL_AXES = ("y", "z", "core", "x")


def make_tables(channel_of, points):
    outer = 64
    inner = points // outer
    step = 2.0 * math.pi / points
    a_index = jnp.arange(inner, dtype=jnp.int32)
    b_index = jnp.arange(outer, dtype=jnp.int32)
    a_turns = (channel_of[:, None] * a_index[None, :] % inner) * outer
    b_turns = channel_of[:, None] * b_index[None, :] % points
    a_angle = a_turns.astype(jnp.float32) * step
    b_angle = b_turns.astype(jnp.float32) * step
    ca, sa = jnp.cos(a_angle)[:, :, None], jnp.sin(a_angle)[:, :, None]
    cb, sb = jnp.cos(b_angle)[:, None, :], jnp.sin(b_angle)[:, None, :]
    table_scale = 1.0 / math.sqrt(points)
    cos_table = ((ca * cb - sa * sb) * table_scale).astype(jnp.bfloat16)
    sin_table = ((sa * cb + ca * sb) * table_scale).astype(jnp.bfloat16)
    slots = channel_of.shape[0]
    return (cos_table.reshape(slots, points), sin_table.reshape(slots, points))


def make_weights(beam_stations, beam_codes, stations):
    station_ids = jnp.arange(stations, dtype=jnp.int32)
    onehot = (beam_stations[:, :, None] == station_ids[None, None, :]).astype(jnp.float32)
    amplitude = (1 + beam_codes // 64).astype(jnp.float32)
    phase_angle = (beam_codes % 64).astype(jnp.float32) * (2.0 * math.pi / 64.0)
    weight_re = jnp.einsum("bk,bks->bs", amplitude * jnp.cos(phase_angle), onehot)
    weight_im = jnp.einsum("bk,bks->bs", amplitude * jnp.sin(phase_angle), onehot)
    return (weight_re.astype(jnp.bfloat16), weight_im.astype(jnp.bfloat16))


def fir_kernel(x_ref, h_ref, o_ref, os_ref):
    tap_count = h_ref.shape[0]
    blocks, rows, lanes = x_ref.shape[1], x_ref.shape[2], x_ref.shape[3]
    inputs_here = o_ref.shape[1]
    spectra = o_ref.shape[2]
    for block in range(blocks):
        taps = [
            jnp.broadcast_to(h_ref[pl.ds(t, 1), pl.ds(block * lanes, lanes)], (rows, lanes))
            for t in range(tap_count)
        ]

        def frame_body(step, carry):
            first = pl.multiple_of(step * 8, 8)
            window = [
                x_ref[first + f, block].astype(jnp.float32) for f in range(8 + tap_count - 1)
            ]
            for k in range(8):
                acc = taps[0] * window[k]
                for t in range(1, tap_count):
                    acc = acc + taps[t] * window[k + t]
                os_ref[pl.ds(first + k, rows, stride=spectra), :] = acc
            return carry

        lax.fori_loop(0, spectra // 8, frame_body, 0)
        for r in range(rows):
            o_ref[r // inputs_here, r % inputs_here, :, pl.ds(block * lanes, lanes)] = os_ref[
                pl.ds(r * spectra, spectra), :
            ].astype(o_ref.dtype)


def polyphase(in_block, fir_taps, spectra):
    tap_count, points = fir_taps.shape
    components, inputs_here, samples = in_block.shape
    rows = components * inputs_here
    lanes = 128
    frames = samples // points
    per_frame = points // lanes
    tiles = in_block.reshape(components, inputs_here, samples // lanes, lanes)
    tiles = jnp.transpose(tiles, (2, 0, 1, 3))
    tiles = tiles.reshape(frames, per_frame, rows, lanes)
    blocks = 2
    return pl.pallas_call(
        fir_kernel,
        grid=(per_frame // blocks,),
        in_specs=[
            pl.BlockSpec((frames, blocks, rows, lanes), lambda b: (0, b, 0, 0)),
            pl.BlockSpec((tap_count, blocks * lanes), lambda b: (0, b)),
        ],
        out_specs=pl.BlockSpec(
            (components, inputs_here, spectra, blocks * lanes), lambda b: (0, 0, 0, b)
        ),
        out_shape=jax.ShapeDtypeStruct((components, inputs_here, spectra, points), jnp.bfloat16),
        scratch_shapes=[pltpu.VMEM((rows * spectra, lanes), jnp.float32)],
    )(tiles, fir_taps)


def contract(left_rows, right_rows):
    contract_dims = (((1,), (1,)), ((), ()))
    return lax.dot_general(left_rows, right_rows, contract_dims, preferred_element_type=jnp.float32)


def spectrum(filtered, cos_table, sin_table, slot_gain):
    inputs_here, spectra, points = (filtered.shape[1], filtered.shape[2], filtered.shape[3])
    rows = inputs_here * spectra
    slots = cos_table.shape[0]
    tables = jnp.concatenate([cos_table, sin_table], axis=0)
    products = contract(tables, filtered.reshape(2 * rows, points))
    cos_re, cos_im = products[:slots, :rows], products[:slots, rows:]
    sin_re, sin_im = products[slots:, :rows], products[slots:, rows:]
    spec_re = cos_re + sin_im
    spec_im = cos_im - sin_re
    combined = jnp.concatenate(
        [spec_re.reshape(-1, inputs_here, spectra), spec_im.reshape(-1, inputs_here, spectra)],
        axis=2,
    )
    return (combined * slot_gain[:, None, None]).astype(jnp.bfloat16)


def form_beams(beam_data, weight_re, weight_im):
    spectra = beam_data.shape[2] // 2
    samples = beam_data.reshape(beam_data.shape[0], -1, 2, beam_data.shape[2])
    with_re = jnp.einsum("bs,jspt->jbpt", weight_re, samples, preferred_element_type=jnp.float32)
    with_im = jnp.einsum("bs,jspt->jbpt", weight_im, samples, preferred_element_type=jnp.float32)
    out_re = with_re[..., :spectra] - with_im[..., spectra:]
    out_im = with_re[..., spectra:] + with_im[..., :spectra]
    return jnp.concatenate([out_re, out_im], axis=3)


def per_device(
    voltages, fir_taps, cor_channels, beam_channels, cor_gain, beam_gain, beam_stations, beam_codes
):
    tap_count, points = fir_taps.shape
    stn_count = lax.axis_size(STN_AXES)
    sec_count = lax.axis_size("x")
    device_count = stn_count * sec_count
    inputs_here = voltages.shape[1]
    spectra = voltages.shape[2] // points - tap_count + 1
    filtered = polyphase(voltages, fir_taps, spectra)
    channel_of = jnp.stack([cor_channels, beam_channels], axis=1).reshape(-1)
    slot_gain = jnp.stack([cor_gain, beam_gain], axis=1).reshape(-1)
    cos_table, sin_table = lax.optimization_barrier(make_tables(channel_of, points))
    weight_re, weight_im = make_weights(beam_stations, beam_codes, STATIONS)
    spectra_all = spectrum(filtered, cos_table, sin_table, slot_gain)
    outgoing = spectra_all.reshape(device_count, 2, inputs_here, 2 * spectra)
    turned = lax.all_to_all(outgoing, ALL_AXES, split_axis=0, concat_axis=0, tiled=True)
    cor_data = turned[:, 0].reshape(device_count * inputs_here, 2 * spectra)
    beam_data = turned[:, 1].reshape(1, device_count * inputs_here, 2 * spectra)
    raw_beams = form_beams(beam_data, weight_re, weight_im)
    local_power = jnp.sum(raw_beams * raw_beams, axis=(0, 2, 3))
    spread_power = jnp.broadcast_to(local_power[None], (device_count, local_power.shape[0]))
    spread_power, cor_data = lax.optimization_barrier((spread_power, cor_data))
    gathered_power = lax.all_to_all(spread_power, ALL_AXES, split_axis=0, concat_axis=0, tiled=True)
    swapped = jnp.concatenate([cor_data[:, spectra:], -cor_data[:, :spectra]], axis=1)
    both = contract(jnp.concatenate([cor_data, swapped], axis=0), cor_data) / spectra
    visibilities = both.reshape(1, 2, cor_data.shape[0], cor_data.shape[0]).astype(jnp.bfloat16)
    summed_power = jnp.sum(gathered_power, axis=0)
    beam_power = summed_power / (device_count * raw_beams.shape[2] * raw_beams.shape[3])
    beams = (raw_beams * lax.rsqrt(beam_power + epsilon)[None, :, None, None]).astype(jnp.bfloat16)
    return (visibilities, beams)


def solution(mesh):
    stn_count, sec_count = mesh.devices.shape
    cores = 2
    y_count = 4
    z_count = stn_count // (y_count * cores)
    devices = mesh.devices.reshape(y_count, z_count, cores, sec_count)
    fine = jax.sharding.Mesh(devices, ("y", "z", "core", "x"))
    spread = ("y", "z", "core", "x")
    in_specs = (P(None, spread, None), P(), P(), P(), P(), P(), P(), P())
    out_specs = (P(spread, None, None, None), P(spread, None, None, None))
    return jax.shard_map(
        per_device, mesh=fine, in_specs=in_specs, out_specs=out_specs, check_vma=False
    )
```
